32 devices in a mesh: grp: 2 (over x), tile: 16 (over z, y, core).
Axes of the slice: x: 2, y: 2, z: 4, core: 2. Of those that a mesh axis runs over, the one named last changes fastest.
Arguments:
- latents: bfloat16 [384, 16, 8, 256], P(('grp', 'tile')), parts along dimension 0, may hold values from -6 to 6
- frame_counts: int32 [32], P('grp'), parts along dimension 0, may hold values from 1 to 12, 64 in all
- clip_order: int32 [32], P('grp'), parts along dimension 0, may hold values from 0 to 15, each once
- norm_scale: float32 [256], replicated, may hold values from 0.25 to 1.75
- norm_offset: float32 [256], replicated, may hold values from -3 to 3
- conv_weight: bfloat16 [3, 3, 3, 256, 256], replicated, may hold values from -0.078125 to 0.078125
- conv_bias: float32 [256], replicated, may hold values from -3 to 3
- out_scale: float32 [256], replicated, may hold values from 0.25 to 1.75
- out_offset: float32 [256], replicated, may hold values from -3 to 3
Outputs:
- block_out: bfloat16 [2, 1024, 8, 256], P(None, ('grp', 'tile')), parts along dimension 1
- normed: bfloat16 [2, 1024, 8, 256], P(None, ('grp', 'tile')), parts along dimension 1
The draws below stay inside these ranges and needn't reach their ends.
There are 2 independent parts, one for each index of `grp`. The reference program is written for one: setup_inputs(seed, part) draws one part's arguments, and reference() takes and returns one part's arrays. A program takes and returns all parts, laid end to end along the dimension named above; an argument that names none is the same for every part. Nothing has to cross between parts.
Inputs may be any that keep to these rules, and one draw needn't show every extreme that they name: `frame_counts`: they sum to 64; the largest is exactly 12. `clip_order`: A permutation of the clips.
All inputs are finite; a program needn't handle non-finite values.
Results may differ from the reference program's by a relative error of at most 0.0057.
Values may be sent and summed in bfloat16 or wider, within the bound.
No kernel may reach another device: no remote copies, remote signals or barrier semaphores. Data moves between devices by JAX's collectives and lax.ppermute only.
A program may use at most 64 MiB of HBM per device.

```python
import math
import jax
import jax.numpy as jnp
import numpy as np
from jax import lax

CH = 256
GROUPS = 32
MEANF = 4
NRB = 8
RB = 2
COLS = 8
MOSTF = 12
ROWS = 16
CLIPS = 16
WT = 32
TILES = 512
N_TILE = 16


def block_scale(own_key, dims, shards, smallest, largest):
    def one(axis_at, blocks):
        heights = jax.random.uniform(jax.random.fold_in(jax.random.fold_in(own_key, 6), axis_at), (blocks,), jnp.float32, smallest / len(shards), largest / len(shards))
        return jnp.repeat(jnp.exp(heights), dims[axis_at] // blocks).reshape((-1,) + (1,) * (len(dims) - axis_at - 1))

    level = one(*shards[0])
    for cut in shards[1:]:
        level = level * one(*cut)
    return level


def split_up(count, total, most, slope):
    portions = [(1 << 20) // math.isqrt(standing ** slope) + 1 for standing in range(2, count + 1)]
    spare, counts = total - most - (count - 1), [1] * (count - 1)
    while spare > 0:
        candidates = [i for i in range(count - 1) if counts[i] < most]
        whole, left = sum([portions[i] for i in candidates]), spare
        for i in candidates:
            extra = min(most - counts[i], max(1, left * portions[i] // whole), spare)
            counts[i] = counts[i] + extra
            spare = spare - extra
    return np.array([most] + counts)


def ragged_sizes(rng, number_of, total, limit, lean):
    if number_of == 2:
        one = jax.random.randint(rng, (), max(1, total - limit), min(limit, total - 1) + 1)
        return jnp.stack([one, total - one])
    lengths = jnp.asarray(split_up(number_of, total, limit, lean), jnp.int32)
    couples = (number_of - 1) // 2
    source_of, taker = lengths[1:1 + 2 * couples:2], lengths[2:2 + 2 * couples:2]
    slack = jnp.minimum(source_of - 1, limit - taker)
    shifted = jax.random.randint(jax.random.fold_in(rng, 1), (couples,), 0, 1 << 20) % (slack + 1)
    lengths = lengths.at[1:1 + 2 * couples:2].set(source_of - shifted).at[2:2 + 2 * couples:2].set(taker + shifted)
    return lengths[jax.random.permutation(jax.random.fold_in(rng, 2), number_of)]


def bell_draw(rng, shape, scale, most, shards=(), kind=jnp.bfloat16):
    factor_of = block_scale(rng, shape, shards, -0.22, 0.18) if shards else 1.0
    array = jax.random.normal(rng, shape, jnp.float32) * scale * factor_of
    return jnp.minimum(jnp.maximum(array, -most), most).astype(kind)


def setup_inputs(seed: int = 0, part: int = 0) -> dict:
    streams_of = jax.random.split(jax.random.key(seed), 10)
    part_splits = jax.random.split(jax.random.fold_in(streams_of[9], part), 10)
    latents = bell_draw(part_splits[0], (CLIPS * MOSTF, ROWS, COLS, CH), 1.0, 6.0, ((0, 16),))
    frame_counts = ragged_sizes(part_splits[1], CLIPS, MEANF * CLIPS, MOSTF, 2).astype(jnp.int32)
    clip_order = jax.random.permutation(part_splits[2], CLIPS).astype(jnp.int32)
    norm_scale = jnp.clip(1.0 + 0.15 * jax.random.normal(streams_of[3], (CH,), jnp.float32), 0.25, 1.75)
    norm_offset = bell_draw(streams_of[4], (CH,), 0.5, 3.0, (), jnp.float32)
    conv_weight = bell_draw(streams_of[5], (3, 3, 3, CH, CH), (27 * CH) ** -0.5, 0.078125)
    conv_bias = bell_draw(streams_of[6], (CH,), 0.5, 3.0, (), jnp.float32)
    out_scale = jnp.clip(1.0 + 0.15 * jax.random.normal(streams_of[7], (CH,), jnp.float32), 0.25, 1.75)
    out_offset = bell_draw(streams_of[8], (CH,), 0.5, 3.0, (), jnp.float32)
    return {"latents": latents, "frame_counts": frame_counts, "clip_order": clip_order, "norm_scale": norm_scale, "norm_offset": norm_offset, "conv_weight": conv_weight, "conv_bias": conv_bias, "out_scale": out_scale, "out_offset": out_offset}


eps = 1e-06

def normalize(values, frame_count, scaling, offsets):
    frames = values.shape[0]
    channels = values.shape[-1]
    grouped = values.reshape(frames, -1, GROUPS, channels // GROUPS)
    live_mask = (jnp.arange(frames) < frame_count).astype(jnp.float32)[:, None, None, None]
    members = frame_count.astype(jnp.float32) * grouped.shape[1] * grouped.shape[3]
    group_mean = lax.optimization_barrier(jnp.sum(grouped * live_mask, axis=(0, 1, 3))) / members
    spread = lax.optimization_barrier(jnp.sum(grouped * grouped * live_mask, axis=(0, 1, 3))) / members - group_mean * group_mean
    inverse = lax.rsqrt(spread + eps)
    normed = (grouped - group_mean[:, None]) * inverse[:, None] * scaling.reshape(GROUPS, -1) + offsets.reshape(GROUPS, -1)
    return jax.nn.silu(normed).reshape(values.shape)

def reference(latents, frame_counts, clip_order, norm_scale, norm_offset, conv_weight, conv_bias, out_scale, out_offset):
    clips = latents.reshape(CLIPS, MOSTF, ROWS, COLS, CH)

    def activate(packed):
        return normalize(packed[0].astype(jnp.float32), packed[1], norm_scale, norm_offset).astype(jnp.bfloat16)
    active = lax.map(activate, (clips, frame_counts))
    padded = jnp.pad(active, ((0, 0), (2, 0), (1, 1), (1, 1), (0, 0)))
    ordered = jnp.take(frame_counts, clip_order).astype(jnp.int32)
    starts = ((jnp.cumsum(ordered) - ordered) * NRB).astype(jnp.int32)
    slot_all = jnp.arange(TILES, dtype=jnp.int32)
    tile_id = (slot_all % WT * N_TILE + slot_all // WT).astype(jnp.int32)
    placed = (lax.optimization_barrier(jnp.sum((starts[None, :] <= tile_id[:, None]).astype(jnp.int32), axis=1)) - 1).astype(jnp.int32)
    clip_id = jnp.take(clip_order, placed).astype(jnp.int32)
    within = (tile_id - jnp.take(starts, placed)).astype(jnp.int32)
    frame_index = (within // NRB).astype(jnp.int32)
    row_band = (within % NRB).astype(jnp.int32)
    kernel = conv_weight.reshape(27 * CH, CH)

    def one_worker(picked):
        clip_part, frame_part, band_part = picked

        def window(clip_one, frame_one, band_one):
            zero = jnp.zeros((), jnp.int32)
            return lax.dynamic_slice(padded, (clip_one, frame_one, band_one * RB, zero, zero), (1, 3, RB + 2, COLS + 2, CH))[0]
        stacks = jax.vmap(window)(clip_part, frame_part, band_part)
        tap_list = [stacks[:, frame_lag, row_tap:row_tap + RB, col_tap:col_tap + COLS] for frame_lag in range(3) for row_tap in range(3) for col_tap in range(3)]
        unfolded = jnp.concatenate(tap_list, axis=-1).reshape(-1, 27 * CH)
        result = jnp.dot(unfolded, kernel, preferred_element_type=jnp.float32) + conv_bias
        return result.astype(jnp.bfloat16).reshape(WT, RB, COLS, CH)
    conv_tiles = lax.map(one_worker, (clip_id.reshape(N_TILE, WT), frame_index.reshape(N_TILE, WT), row_band.reshape(N_TILE, WT)))
    conv_flat = conv_tiles.reshape(TILES, RB, COLS, CH)
    per_group = CH // GROUPS
    grouped = conv_flat.astype(jnp.float32).reshape(TILES, RB * COLS, GROUPS, per_group)
    first_sum = jax.ops.segment_sum(lax.optimization_barrier(jnp.sum(grouped, axis=(1, 3))), clip_id, CLIPS)
    second_sum = jax.ops.segment_sum(lax.optimization_barrier(jnp.sum(grouped * grouped, axis=(1, 3))), clip_id, CLIPS)
    members = frame_counts.astype(jnp.float32) * (ROWS * COLS * per_group)
    clip_mean = first_sum / members[:, None]
    clip_spread = second_sum / members[:, None] - clip_mean * clip_mean
    clip_inverse = lax.rsqrt(clip_spread + eps)
    tile_mean = jnp.take(clip_mean, clip_id, axis=0)
    tile_inverse = jnp.take(clip_inverse, clip_id, axis=0)
    normed = (grouped - tile_mean[:, None, :, None]) * tile_inverse[:, None, :, None] * out_scale.reshape(GROUPS, per_group) + out_offset.reshape(GROUPS, per_group)
    normed = jax.nn.silu(normed).astype(jnp.bfloat16).reshape(TILES, RB, COLS, CH)
    return (jnp.transpose(conv_flat, (1, 0, 2, 3)), jnp.transpose(normed, (1, 0, 2, 3)))
```

```python
import jax
import jax.numpy as jnp
from jax import lax
from jax.sharding import PartitionSpec as P

GROUPS = 32
MEANF = 4
NRB = 8


eps = 1e-06


def normalize(values, frame_count, scaling, offsets):
    frames = values.shape[0]
    channels = values.shape[-1]
    grouped = values.reshape(frames, -1, GROUPS, channels // GROUPS)
    live_mask = (jnp.arange(frames) < frame_count).astype(jnp.float32)[:, None, None, None]
    members = frame_count.astype(jnp.float32) * grouped.shape[1] * grouped.shape[3]
    group_mean = jnp.sum(grouped * live_mask, axis=(0, 1, 3)) / members
    spread = (
        jnp.sum(grouped * grouped * live_mask, axis=(0, 1, 3)) / members - group_mean * group_mean
    )
    inverse = lax.rsqrt(spread + eps)
    normed = (grouped - group_mean[:, None]) * inverse[:, None] * scaling.reshape(
        GROUPS, -1
    ) + offsets.reshape(GROUPS, -1)
    return jax.nn.silu(normed).reshape(values.shape)


def local(
    latents,
    frame_counts,
    clip_order,
    norm_scale,
    norm_offset,
    conv_weight,
    conv_bias,
    out_scale,
    out_offset,
):
    devices = lax.axis_size("tile")
    device = lax.axis_index("tile")
    frames, frame_rows, columns, channels = latents.shape
    tile_rows = frame_rows // NRB
    classes = devices // NRB
    per_dest = (frames + classes - 1) // classes
    worker_tiles = MEANF * NRB
    positions = jnp.arange(frame_counts.shape[0], dtype=jnp.int32)
    chosen = clip_order[:, None] == positions[None, :]
    ordered = jnp.sum(jnp.where(chosen, frame_counts[None, :], 0), axis=1)
    starts = (jnp.cumsum(ordered) - ordered) * NRB
    own_start = jnp.sum(jnp.where(clip_order == device, starts, 0))
    own_count = jnp.sum(jnp.where(positions == device, frame_counts, 0))

    active = normalize(latents.astype(jnp.float32), own_count, norm_scale, norm_offset).astype(
        jnp.bfloat16
    )
    conv = lax.conv_general_dilated(
        active[None],
        conv_weight,
        window_strides=(1, 1, 1),
        padding=((2, 0), (1, 1), (1, 1)),
        dimension_numbers=("NDHWC", "DHWIO", "NDHWC"),
        preferred_element_type=jnp.float32,
    )[0]
    block_out = (conv + conv_bias).astype(jnp.bfloat16)
    per_group = channels // GROUPS
    grouped = block_out.astype(jnp.float32).reshape(frames, frame_rows * columns, GROUPS, per_group)
    live_mask = (jnp.arange(frames) < own_count).astype(jnp.float32)[:, None, None, None]
    members = own_count.astype(jnp.float32) * (frame_rows * columns * per_group)
    first_sum = jnp.sum(grouped * live_mask, axis=(0, 1, 3))
    second_sum = jnp.sum(grouped * grouped * live_mask, axis=(0, 1, 3))
    clip_mean = first_sum / members
    clip_spread = second_sum / members - clip_mean * clip_mean
    clip_inverse = lax.rsqrt(clip_spread + eps)
    normed = (grouped - clip_mean[:, None]) * clip_inverse[:, None] * out_scale.reshape(
        GROUPS, per_group
    ) + out_offset.reshape(GROUPS, per_group)
    normed = jax.nn.silu(normed).astype(jnp.bfloat16).reshape(block_out.shape)

    both = jnp.stack([block_out, normed], 0).reshape(
        2, frames, NRB, tile_rows, columns, channels
    )
    both = jnp.pad(both, ((0, 0), (0, per_dest * classes - frames), (0, 0), (0, 0), (0, 0), (0, 0)))
    both = both.reshape(2, per_dest, classes, NRB, tile_rows, columns, channels)
    shift = own_start // NRB
    pick = (jnp.arange(classes, dtype=jnp.int32) - shift) % classes
    both = jnp.take(both, pick, axis=2)
    outgoing = jnp.transpose(both, (2, 3, 1, 0, 4, 5, 6)).reshape(
        devices, per_dest, 2, tile_rows, columns, channels
    )
    received = lax.all_to_all(outgoing, "tile", split_axis=0, concat_axis=0, tiled=True)
    received = received.reshape(devices * per_dest, 2, tile_rows, columns, channels)

    local_slot = jnp.arange(worker_tiles, dtype=jnp.int32)
    tile_id = local_slot * devices + device
    placed = jnp.sum((starts[None, :] <= tile_id[:, None]).astype(jnp.int32), axis=1) - 1
    at_place = placed[:, None] == positions[None, :]
    clip_id = jnp.sum(jnp.where(at_place, clip_order[None, :], 0), axis=1)
    within = tile_id - jnp.sum(jnp.where(at_place, starts[None, :], 0), axis=1)
    take_from = clip_id * per_dest + within // NRB // classes
    mine = jnp.take(received, take_from, axis=0)
    mine = jnp.transpose(mine, (1, 2, 0, 3, 4))
    return (mine[0], mine[1])


def solution(mesh):
    in_specs = (
        P(("grp", "tile"), None, None, None),
        P("grp"),
        P("grp"),
        P(),
        P(),
        P(),
        P(),
        P(),
        P(),
    )
    out_specs = (P(None, ("grp", "tile"), None, None), P(None, ("grp", "tile"), None, None))
    return jax.shard_map(local, mesh=mesh, in_specs=in_specs, out_specs=out_specs, check_vma=False)
```

```python
import jax
import jax.numpy as jnp
from jax import lax
from jax.sharding import PartitionSpec as P

GROUPS = 32
MEANF = 4
NRB = 8


eps = 1e-06


def normalize(values, frame_count, scaling, offsets):
    frames = values.shape[0]
    channels = values.shape[-1]
    grouped = values.reshape(frames, -1, GROUPS, channels // GROUPS)
    live_mask = (jnp.arange(frames) < frame_count).astype(jnp.float32)[:, None, None, None]
    members = frame_count.astype(jnp.float32) * grouped.shape[1] * grouped.shape[3]
    group_mean = jnp.sum(grouped * live_mask, axis=(0, 1, 3)) / members
    spread = (
        jnp.sum(grouped * grouped * live_mask, axis=(0, 1, 3)) / members - group_mean * group_mean
    )
    inverse = lax.rsqrt(spread + eps)
    normed = (grouped - group_mean[:, None]) * inverse[:, None] * scaling.reshape(
        GROUPS, -1
    ) + offsets.reshape(GROUPS, -1)
    return jax.nn.silu(normed).reshape(values.shape)


def local(
    latents,
    frame_counts,
    clip_order,
    norm_scale,
    norm_offset,
    conv_weight,
    conv_bias,
    out_scale,
    out_offset,
):
    devices = lax.axis_size("tile")
    device = lax.axis_index("tile")
    frames, frame_rows, columns, channels = latents.shape
    tile_rows = frame_rows // NRB
    classes = devices // NRB
    per_dest = (frames + classes - 1) // classes
    worker_tiles = MEANF * NRB
    positions = jnp.arange(frame_counts.shape[0], dtype=jnp.int32)
    chosen = clip_order[:, None] == positions[None, :]
    ordered = jnp.sum(jnp.where(chosen, frame_counts[None, :], 0), axis=1)
    starts = (jnp.cumsum(ordered) - ordered) * NRB
    own_start = jnp.sum(jnp.where(clip_order == device, starts, 0))
    own_count = jnp.sum(jnp.where(positions == device, frame_counts, 0))

    active = normalize(latents.astype(jnp.float32), own_count, norm_scale, norm_offset).astype(
        jnp.bfloat16
    )
    padded = jnp.pad(active, ((2, 0), (1, 1), (1, 1), (0, 0)))
    unfolded = jnp.concatenate(
        [
            padded[:, row_tap : row_tap + frame_rows, col_tap : col_tap + columns]
            for row_tap in range(3)
            for col_tap in range(3)
        ],
        axis=-1,
    ).reshape(frames + 2, frame_rows * columns, 9 * channels)
    kernel = conv_weight.reshape(3, 9 * channels, -1)
    conv = conv_bias + sum(
        jnp.dot(
            unfolded[frame_lag : frame_lag + frames].reshape(-1, 9 * channels),
            kernel[frame_lag],
            preferred_element_type=jnp.float32,
        )
        for frame_lag in range(3)
    ).reshape(frames, frame_rows, columns, -1)
    block_out = conv.astype(jnp.bfloat16)
    per_group = channels // GROUPS
    grouped = block_out.astype(jnp.float32).reshape(frames, frame_rows * columns, GROUPS, per_group)
    live_mask = (jnp.arange(frames) < own_count).astype(jnp.float32)[:, None, None, None]
    members = own_count.astype(jnp.float32) * (frame_rows * columns * per_group)
    first_sum = jnp.sum(grouped * live_mask, axis=(0, 1, 3))
    second_sum = jnp.sum(grouped * grouped * live_mask, axis=(0, 1, 3))
    clip_mean = first_sum / members
    clip_spread = second_sum / members - clip_mean * clip_mean
    clip_inverse = lax.rsqrt(clip_spread + eps)
    normed = (grouped - clip_mean[:, None]) * clip_inverse[:, None] * out_scale.reshape(
        GROUPS, per_group
    ) + out_offset.reshape(GROUPS, per_group)
    normed = jax.nn.silu(normed).astype(jnp.bfloat16).reshape(block_out.shape)

    both = jnp.stack([block_out, normed], 0).reshape(
        2, frames, NRB, tile_rows, columns, channels
    )
    both = jnp.pad(both, ((0, 0), (0, per_dest * classes - frames), (0, 0), (0, 0), (0, 0), (0, 0)))
    both = both.reshape(2, per_dest, classes, NRB, tile_rows, columns, channels)
    shift = own_start // NRB
    pick = (jnp.arange(classes, dtype=jnp.int32) - shift) % classes
    both = jnp.take(both, pick, axis=2)
    outgoing = jnp.transpose(both, (2, 3, 1, 0, 4, 5, 6)).reshape(
        devices, per_dest, 2, tile_rows, columns, channels
    )
    received = lax.all_to_all(outgoing, "tile", split_axis=0, concat_axis=0, tiled=True)
    received = received.reshape(devices * per_dest, 2, tile_rows, columns, channels)

    local_slot = jnp.arange(worker_tiles, dtype=jnp.int32)
    tile_id = local_slot * devices + device
    placed = jnp.sum((starts[None, :] <= tile_id[:, None]).astype(jnp.int32), axis=1) - 1
    at_place = placed[:, None] == positions[None, :]
    clip_id = jnp.sum(jnp.where(at_place, clip_order[None, :], 0), axis=1)
    within = tile_id - jnp.sum(jnp.where(at_place, starts[None, :], 0), axis=1)
    take_from = clip_id * per_dest + within // NRB // classes
    mine = jnp.take(received, take_from, axis=0)
    mine = jnp.transpose(mine, (1, 2, 0, 3, 4))
    return (mine[0], mine[1])


def solution(mesh):
    in_specs = (
        P(("grp", "tile"), None, None, None),
        P("grp"),
        P("grp"),
        P(),
        P(),
        P(),
        P(),
        P(),
        P(),
    )
    out_specs = (P(None, ("grp", "tile"), None, None), P(None, ("grp", "tile"), None, None))
    return jax.shard_map(local, mesh=mesh, in_specs=in_specs, out_specs=out_specs, check_vma=False)
```

```python
import jax
import jax.numpy as jnp
from jax import lax
from jax.sharding import PartitionSpec as P

GROUPS = 32
MEANF = 4
NRB = 8


eps = 1e-06


def normalize(values, frame_count, scaling, offsets):
    frames = values.shape[0]
    channels = values.shape[-1]
    grouped = values.reshape(frames, -1, GROUPS, channels // GROUPS)
    live_mask = (jnp.arange(frames) < frame_count).astype(jnp.float32)[:, None, None, None]
    members = frame_count.astype(jnp.float32) * grouped.shape[1] * grouped.shape[3]
    group_mean = jnp.sum(grouped * live_mask, axis=(0, 1, 3)) / members
    spread = (
        jnp.sum(grouped * grouped * live_mask, axis=(0, 1, 3)) / members - group_mean * group_mean
    )
    inverse = lax.rsqrt(spread + eps)
    normed = (grouped - group_mean[:, None]) * inverse[:, None] * scaling.reshape(
        GROUPS, -1
    ) + offsets.reshape(GROUPS, -1)
    return jax.nn.silu(normed).reshape(values.shape)


def local(
    latents,
    frame_counts,
    clip_order,
    norm_scale,
    norm_offset,
    conv_weight,
    conv_bias,
    out_scale,
    out_offset,
):
    devices = lax.axis_size("tile")
    device = lax.axis_index("tile")
    frames, frame_rows, columns, channels = latents.shape
    tile_rows = frame_rows // NRB
    classes = devices // NRB
    per_dest = (frames + classes - 1) // classes
    worker_tiles = MEANF * NRB
    positions = jnp.arange(frame_counts.shape[0], dtype=jnp.int32)
    chosen = clip_order[:, None] == positions[None, :]
    ordered = jnp.sum(jnp.where(chosen, frame_counts[None, :], 0), axis=1)
    starts = (jnp.cumsum(ordered) - ordered) * NRB
    own_start = jnp.sum(jnp.where(clip_order == device, starts, 0))
    own_count = jnp.sum(jnp.where(positions == device, frame_counts, 0))

    active = normalize(latents.astype(jnp.float32), own_count, norm_scale, norm_offset).astype(
        jnp.bfloat16
    )
    padded = jnp.pad(active, ((2, 0), (1, 1), (1, 1), (0, 0)))
    unfolded = jnp.concatenate(
        [
            padded[:, row_tap : row_tap + frame_rows, col_tap : col_tap + columns]
            for row_tap in range(3)
            for col_tap in range(3)
        ],
        axis=-1,
    ).reshape(frames + 2, frame_rows * columns, 9 * channels)
    kernel = conv_weight.reshape(3, 9 * channels, -1)
    conv = conv_bias + sum(
        jnp.dot(
            unfolded[frame_lag : frame_lag + frames].reshape(-1, 9 * channels),
            kernel[frame_lag],
            preferred_element_type=jnp.float32,
        )
        for frame_lag in range(3)
    ).reshape(frames, frame_rows, columns, -1)
    block_out = conv.astype(jnp.bfloat16)
    per_group = channels // GROUPS
    grouped = block_out.astype(jnp.float32).reshape(frames, frame_rows * columns, GROUPS, per_group)
    live_mask = (jnp.arange(frames) < own_count).astype(jnp.float32)[:, None, None, None]
    members = own_count.astype(jnp.float32) * (frame_rows * columns * per_group)
    first_sum = jnp.sum(grouped * live_mask, axis=(0, 1, 3))
    second_sum = jnp.sum(grouped * grouped * live_mask, axis=(0, 1, 3))
    clip_mean = first_sum / members
    clip_spread = second_sum / members - clip_mean * clip_mean
    clip_inverse = lax.rsqrt(clip_spread + eps)

    tiles = block_out.reshape(frames, NRB, tile_rows, columns, channels)
    tiles = jnp.pad(tiles, ((0, per_dest * classes - frames), (0, 0), (0, 0), (0, 0), (0, 0)))
    tiles = tiles.reshape(per_dest, classes, NRB, tile_rows, columns, channels)
    shift = own_start // NRB
    pick = (jnp.arange(classes, dtype=jnp.int32) - shift) % classes
    tiles = jnp.take(tiles, pick, axis=1)
    tiles = jnp.transpose(tiles, (1, 2, 0, 3, 4, 5)).reshape(
        devices, per_dest * tile_rows * columns, channels
    )
    stats = jnp.stack([clip_mean, clip_inverse], 0)
    stats = jnp.repeat(stats, per_group, axis=1)
    high = lax.reduce_precision(stats, exponent_bits=8, mantissa_bits=7)
    low = stats - high
    stat_rows = jnp.concatenate([high, low, jnp.zeros((4, channels), jnp.float32)], 0)
    stat_rows = jnp.broadcast_to(stat_rows.astype(jnp.bfloat16)[None], (devices, 8, channels))
    outgoing = jnp.concatenate([tiles, stat_rows], 1)
    received = lax.all_to_all(outgoing, "tile", split_axis=0, concat_axis=0, tiled=True)
    block_part = received[:, : per_dest * tile_rows * columns].reshape(
        devices * per_dest, tile_rows, columns, channels
    )
    stat_part = received[:, per_dest * tile_rows * columns :].astype(jnp.float32)
    src_mean = stat_part[:, 0] + stat_part[:, 2]
    src_inverse = stat_part[:, 1] + stat_part[:, 3]

    local_slot = jnp.arange(worker_tiles, dtype=jnp.int32)
    tile_id = local_slot * devices + device
    placed = jnp.sum((starts[None, :] <= tile_id[:, None]).astype(jnp.int32), axis=1) - 1
    at_place = placed[:, None] == positions[None, :]
    clip_id = jnp.sum(jnp.where(at_place, clip_order[None, :], 0), axis=1)
    within = tile_id - jnp.sum(jnp.where(at_place, starts[None, :], 0), axis=1)
    take_from = clip_id * per_dest + within // NRB // classes
    mine = jnp.take(block_part, take_from, axis=0)
    tile_mean = jnp.take(src_mean, clip_id, axis=0)
    tile_inverse = jnp.take(src_inverse, clip_id, axis=0)
    normed = (mine.astype(jnp.float32) - tile_mean[:, None, None, :]) * tile_inverse[
        :, None, None, :
    ] * out_scale + out_offset
    normed = jax.nn.silu(normed).astype(jnp.bfloat16)
    return (jnp.transpose(mine, (1, 0, 2, 3)), jnp.transpose(normed, (1, 0, 2, 3)))


def solution(mesh):
    in_specs = (
        P(("grp", "tile"), None, None, None),
        P("grp"),
        P("grp"),
        P(),
        P(),
        P(),
        P(),
        P(),
        P(),
    )
    out_specs = (P(None, ("grp", "tile"), None, None), P(None, ("grp", "tile"), None, None))
    return jax.shard_map(local, mesh=mesh, in_specs=in_specs, out_specs=out_specs, check_vma=False)
```

```python
import jax
import jax.numpy as jnp
from jax import lax
from jax.sharding import PartitionSpec as P

GROUPS = 32
MEANF = 4
NRB = 8


eps = 1e-06


def normalize(values, frame_count, scaling, offsets):
    frames = values.shape[0]
    channels = values.shape[-1]
    grouped = values.reshape(frames, -1, GROUPS, channels // GROUPS)
    live_mask = (jnp.arange(frames) < frame_count).astype(jnp.float32)[:, None, None, None]
    members = frame_count.astype(jnp.float32) * grouped.shape[1] * grouped.shape[3]
    group_mean = jnp.sum(grouped * live_mask, axis=(0, 1, 3)) / members
    spread = (
        jnp.sum(grouped * grouped * live_mask, axis=(0, 1, 3)) / members - group_mean * group_mean
    )
    inverse = lax.rsqrt(spread + eps)
    normed = (grouped - group_mean[:, None]) * inverse[:, None] * scaling.reshape(
        GROUPS, -1
    ) + offsets.reshape(GROUPS, -1)
    return jax.nn.silu(normed).reshape(values.shape)


def local(
    latents,
    frame_counts,
    clip_order,
    norm_scale,
    norm_offset,
    conv_weight,
    conv_bias,
    out_scale,
    out_offset,
):
    devices = lax.axis_size("tile")
    device = lax.axis_index("tile")
    frames, frame_rows, columns, channels = latents.shape
    tile_rows = frame_rows // NRB
    classes = devices // NRB
    per_dest = (frames + classes - 1) // classes
    worker_tiles = MEANF * NRB
    positions = jnp.arange(frame_counts.shape[0], dtype=jnp.int32)
    chosen = clip_order[:, None] == positions[None, :]
    ordered = jnp.sum(jnp.where(chosen, frame_counts[None, :], 0), axis=1)
    starts = (jnp.cumsum(ordered) - ordered) * NRB
    own_start = jnp.sum(jnp.where(clip_order == device, starts, 0))
    own_count = jnp.sum(jnp.where(positions == device, frame_counts, 0))

    active = normalize(latents.astype(jnp.float32), own_count, norm_scale, norm_offset).astype(
        jnp.bfloat16
    )
    padded = jnp.pad(active, ((2, 0), (1, 1), (1, 1), (0, 0)))
    unfolded = jnp.concatenate(
        [
            padded[:, row_tap : row_tap + frame_rows, col_tap : col_tap + columns]
            for row_tap in range(3)
            for col_tap in range(3)
        ],
        axis=-1,
    ).reshape(frames + 2, frame_rows * columns, 9 * channels)
    kernel = conv_weight.reshape(3, 9 * channels, -1)
    conv = conv_bias + sum(
        jnp.dot(
            unfolded[frame_lag : frame_lag + frames].reshape(-1, 9 * channels),
            kernel[frame_lag],
            preferred_element_type=jnp.float32,
        )
        for frame_lag in range(3)
    ).reshape(frames, frame_rows, columns, -1)
    block_out = conv.astype(jnp.bfloat16)
    per_group = channels // GROUPS
    grouped = block_out.astype(jnp.float32).reshape(frames, frame_rows * columns, GROUPS, per_group)
    live_mask = (jnp.arange(frames) < own_count).astype(jnp.float32)[:, None, None, None]
    members = own_count.astype(jnp.float32) * (frame_rows * columns * per_group)
    first_sum = jnp.sum(grouped * live_mask, axis=(0, 1, 3))
    second_sum = jnp.sum(grouped * grouped * live_mask, axis=(0, 1, 3))
    clip_mean = first_sum / members
    clip_spread = second_sum / members - clip_mean * clip_mean
    clip_inverse = lax.rsqrt(clip_spread + eps)

    tiles = block_out.reshape(frames, NRB, tile_rows, columns, channels)
    tiles = jnp.pad(tiles, ((0, per_dest * classes - frames), (0, 0), (0, 0), (0, 0), (0, 0)))
    tiles = tiles.reshape(per_dest, classes, NRB, tile_rows, columns, channels)
    shift = own_start // NRB
    pick = (jnp.arange(classes, dtype=jnp.int32) - shift) % classes
    tiles = jnp.take(tiles, pick, axis=1)
    tiles = jnp.transpose(tiles, (1, 2, 0, 3, 4, 5)).reshape(
        devices, per_dest * tile_rows * columns, channels
    )
    stats = jnp.stack([clip_mean, clip_inverse], 0)
    stats = jnp.repeat(stats, per_group, axis=1)
    high = lax.reduce_precision(stats, exponent_bits=8, mantissa_bits=7)
    low = stats - high
    stat_rows = jnp.concatenate([high, low, jnp.zeros((4, channels), jnp.float32)], 0)
    stat_rows = jnp.broadcast_to(stat_rows.astype(jnp.bfloat16)[None], (devices, 8, channels))
    outgoing = jnp.concatenate([tiles, stat_rows], 1)
    arrived = [None] * devices
    for step in range(devices):
        block = jnp.take(outgoing, (device + step) % devices, axis=0)
        if step:
            block = lax.ppermute(
                block, "tile", [(src, (src + step) % devices) for src in range(devices)]
            )
        arrived[step] = block
    by_step = jnp.stack(arrived, 0)
    received = jnp.take(by_step, (device - jnp.arange(devices)) % devices, axis=0)
    block_part = received[:, : per_dest * tile_rows * columns].reshape(
        devices * per_dest, tile_rows, columns, channels
    )
    stat_part = received[:, per_dest * tile_rows * columns :].astype(jnp.float32)
    src_mean = stat_part[:, 0] + stat_part[:, 2]
    src_inverse = stat_part[:, 1] + stat_part[:, 3]

    local_slot = jnp.arange(worker_tiles, dtype=jnp.int32)
    tile_id = local_slot * devices + device
    placed = jnp.sum((starts[None, :] <= tile_id[:, None]).astype(jnp.int32), axis=1) - 1
    at_place = placed[:, None] == positions[None, :]
    clip_id = jnp.sum(jnp.where(at_place, clip_order[None, :], 0), axis=1)
    within = tile_id - jnp.sum(jnp.where(at_place, starts[None, :], 0), axis=1)
    take_from = clip_id * per_dest + within // NRB // classes
    mine = jnp.take(block_part, take_from, axis=0)
    tile_mean = jnp.take(src_mean, clip_id, axis=0)
    tile_inverse = jnp.take(src_inverse, clip_id, axis=0)
    normed = (mine.astype(jnp.float32) - tile_mean[:, None, None, :]) * tile_inverse[
        :, None, None, :
    ] * out_scale + out_offset
    normed = jax.nn.silu(normed).astype(jnp.bfloat16)
    return (jnp.transpose(mine, (1, 0, 2, 3)), jnp.transpose(normed, (1, 0, 2, 3)))


def solution(mesh):
    in_specs = (
        P(("grp", "tile"), None, None, None),
        P("grp"),
        P("grp"),
        P(),
        P(),
        P(),
        P(),
        P(),
        P(),
    )
    out_specs = (P(None, ("grp", "tile"), None, None), P(None, ("grp", "tile"), None, None))
    return jax.shard_map(local, mesh=mesh, in_specs=in_specs, out_specs=out_specs, check_vma=False)
```

```python
import jax
import jax.numpy as jnp
from jax import lax
from jax.experimental import pallas as pl
from jax.experimental.pallas import tpu as pltpu
from jax.sharding import PartitionSpec as P

GROUPS = 32
MEANF = 4
NRB = 8


eps = 1e-06


def normalize(values, frame_count, scaling, offsets):
    frames = values.shape[0]
    channels = values.shape[-1]
    flat = values.reshape(frames, -1, channels)
    live_mask = (jnp.arange(frames) < frame_count).astype(jnp.float32)[:, None]
    members = frame_count.astype(jnp.float32) * flat.shape[1] * (channels // GROUPS)
    first = jnp.sum(jnp.sum(flat, axis=1) * live_mask, axis=0)
    second = jnp.sum(jnp.sum(flat * flat, axis=1) * live_mask, axis=0)
    group_mean = jnp.sum(first.reshape(GROUPS, -1), axis=1) / members
    spread = jnp.sum(second.reshape(GROUPS, -1), axis=1) / members - group_mean * group_mean
    inverse = lax.rsqrt(spread + eps)
    grouped = values.reshape(frames, -1, GROUPS, channels // GROUPS)
    normed = (grouped - group_mean[:, None]) * inverse[:, None] * scaling.reshape(
        GROUPS, -1
    ) + offsets.reshape(GROUPS, -1)
    return jax.nn.silu(normed).reshape(values.shape)


def conv_body(x_ref, w_ref, b_ref, o_ref, s1_ref, s2_ref):
    step = 2
    positions = x_ref.shape[1]

    def one(j, carry):
        frame = pl.multiple_of(j * step, step)
        acc = jnp.broadcast_to(b_ref[...], (step * positions, o_ref.shape[-1]))
        for frame_lag in range(3):
            lhs = x_ref[pl.ds(frame + frame_lag, step)].reshape(step * positions, -1)
            acc = acc + jnp.dot(lhs, w_ref[frame_lag], preferred_element_type=jnp.float32)
        out = acc.astype(jnp.bfloat16)
        o_ref[pl.ds(frame, step)] = out.reshape(step, positions, -1)
        value = out.astype(jnp.float32).reshape(step, positions, -1)
        s1_ref[pl.ds(frame, step)] = jnp.sum(value, axis=1, keepdims=True)
        s2_ref[pl.ds(frame, step)] = jnp.sum(value * value, axis=1, keepdims=True)
        return carry

    lax.fori_loop(0, o_ref.shape[0] // step, one, 0)


def conv_call(unfolded, kernel, bias):
    frames = unfolded.shape[0] - 2
    positions, width = unfolded.shape[1], unfolded.shape[2]
    channels = kernel.shape[-1]
    vmem = pl.BlockSpec(memory_space=pltpu.VMEM)
    return pl.pallas_call(
        conv_body,
        out_shape=(
            jax.ShapeDtypeStruct((frames, positions, channels), jnp.bfloat16),
            jax.ShapeDtypeStruct((frames, 1, channels), jnp.float32),
            jax.ShapeDtypeStruct((frames, 1, channels), jnp.float32),
        ),
        in_specs=[vmem, vmem, vmem],
        out_specs=(vmem, vmem, vmem),
        cost_estimate=pl.CostEstimate(
            flops=2 * frames * positions * 3 * width * channels,
            transcendentals=0,
            bytes_accessed=unfolded.size * 2 + kernel.size * 2 + frames * positions * channels * 2,
        ),
    )(unfolded, kernel, bias.reshape(1, channels))


def local(
    latents,
    frame_counts,
    clip_order,
    norm_scale,
    norm_offset,
    conv_weight,
    conv_bias,
    out_scale,
    out_offset,
):
    devices = lax.axis_size("tile")
    device = lax.axis_index("tile")
    frames, frame_rows, columns, channels = latents.shape
    tile_rows = frame_rows // NRB
    classes = devices // NRB
    per_dest = (frames + classes - 1) // classes
    worker_tiles = MEANF * NRB
    positions = jnp.arange(frame_counts.shape[0], dtype=jnp.int32)
    chosen = clip_order[:, None] == positions[None, :]
    ordered = jnp.sum(jnp.where(chosen, frame_counts[None, :], 0), axis=1)
    starts = (jnp.cumsum(ordered) - ordered) * NRB
    own_start = jnp.sum(jnp.where(clip_order == device, starts, 0))
    own_count = jnp.sum(jnp.where(positions == device, frame_counts, 0))

    active = normalize(latents.astype(jnp.float32), own_count, norm_scale, norm_offset).astype(
        jnp.bfloat16
    )
    padded = jnp.pad(active, ((2, 0), (1, 1), (1, 1), (0, 0)))
    unfolded = jnp.concatenate(
        [
            padded[:, row_tap : row_tap + frame_rows, col_tap : col_tap + columns]
            for row_tap in range(3)
            for col_tap in range(3)
        ],
        axis=-1,
    ).reshape(frames + 2, frame_rows * columns, 9 * channels)
    kernel = conv_weight.reshape(3, 9 * channels, -1)
    block_out, frame_first, frame_second = conv_call(unfolded, kernel, conv_bias)
    frame_first = frame_first[:, 0]
    frame_second = frame_second[:, 0]
    block_out = block_out.reshape(frames, frame_rows, columns, channels)
    per_group = channels // GROUPS
    live_mask = (jnp.arange(frames) < own_count).astype(jnp.float32)[:, None]
    members = own_count.astype(jnp.float32) * (frame_rows * columns * per_group)
    first_sum = jnp.sum(jnp.sum(frame_first * live_mask, axis=0).reshape(GROUPS, per_group), axis=1)
    second_sum = jnp.sum(jnp.sum(frame_second * live_mask, axis=0).reshape(GROUPS, per_group), axis=1)
    clip_mean = first_sum / members
    clip_spread = second_sum / members - clip_mean * clip_mean
    clip_inverse = lax.rsqrt(clip_spread + eps)

    tiles = block_out.reshape(frames, NRB, tile_rows, columns, channels)
    tiles = jnp.pad(tiles, ((0, per_dest * classes - frames), (0, 0), (0, 0), (0, 0), (0, 0)))
    tiles = tiles.reshape(per_dest, classes, NRB, tile_rows, columns, channels)
    lag_of = (jnp.arange(classes, dtype=jnp.int32)[:, None] - (starts // NRB)[None, :] % classes) % classes
    pick = jnp.sum(jnp.where(clip_order[None, :] == device, lag_of, 0), axis=1)
    tiles = jnp.take(tiles, pick, axis=1)
    tiles = jnp.transpose(tiles, (1, 2, 0, 3, 4, 5)).reshape(
        devices, per_dest * tile_rows * columns, channels
    )
    stats = jnp.stack([clip_mean, clip_inverse], 0)
    stats = jnp.repeat(stats, per_group, axis=1)
    high = lax.reduce_precision(stats, exponent_bits=8, mantissa_bits=7)
    low = stats - high
    stat_rows = jnp.concatenate([high, low, jnp.zeros((4, channels), jnp.float32)], 0)
    stat_rows = jnp.broadcast_to(stat_rows.astype(jnp.bfloat16)[None], (devices, 8, channels))
    outgoing = jnp.concatenate([tiles, stat_rows], 1)
    received = lax.all_to_all(outgoing, "tile", split_axis=0, concat_axis=0, tiled=True)
    block_part = received[:, : per_dest * tile_rows * columns].reshape(
        devices * per_dest, tile_rows, columns, channels
    )
    stat_part = received[:, per_dest * tile_rows * columns :].astype(jnp.float32)
    src_mean = stat_part[:, 0] + stat_part[:, 2]
    src_inverse = stat_part[:, 1] + stat_part[:, 3]

    local_slot = jnp.arange(worker_tiles, dtype=jnp.int32)
    tile_id = local_slot * devices + device
    placed = jnp.sum((starts[None, :] <= tile_id[:, None]).astype(jnp.int32), axis=1) - 1
    at_place = placed[:, None] == positions[None, :]
    clip_id = jnp.sum(jnp.where(at_place, clip_order[None, :], 0), axis=1)
    within = tile_id - jnp.sum(jnp.where(at_place, starts[None, :], 0), axis=1)
    take_from = clip_id * per_dest + within // NRB // classes
    mine = jnp.take(block_part, take_from, axis=0)
    tile_mean = jnp.take(src_mean, clip_id, axis=0)
    tile_inverse = jnp.take(src_inverse, clip_id, axis=0)
    normed = (mine.astype(jnp.float32) - tile_mean[:, None, None, :]) * tile_inverse[
        :, None, None, :
    ] * out_scale + out_offset
    normed = jax.nn.silu(normed).astype(jnp.bfloat16)
    return (jnp.transpose(mine, (1, 0, 2, 3)), jnp.transpose(normed, (1, 0, 2, 3)))


def solution(mesh):
    in_specs = (
        P(("grp", "tile"), None, None, None),
        P("grp"),
        P("grp"),
        P(),
        P(),
        P(),
        P(),
        P(),
        P(),
    )
    out_specs = (P(None, ("grp", "tile"), None, None), P(None, ("grp", "tile"), None, None))
    return jax.shard_map(local, mesh=mesh, in_specs=in_specs, out_specs=out_specs, check_vma=False)
```

```python
import jax
import jax.numpy as jnp
from jax import lax
from jax.sharding import PartitionSpec as P

GROUPS = 32
MEANF = 4
NRB = 8


eps = 1e-06


def normalize(values, frame_count, scaling, offsets):
    frames = values.shape[0]
    channels = values.shape[-1]
    flat = values.reshape(frames, -1, channels)
    live_mask = (jnp.arange(frames) < frame_count).astype(jnp.float32)[:, None]
    members = frame_count.astype(jnp.float32) * flat.shape[1] * (channels // GROUPS)
    first = jnp.sum(jnp.sum(flat, axis=1) * live_mask, axis=0)
    second = jnp.sum(jnp.sum(flat * flat, axis=1) * live_mask, axis=0)
    group_mean = jnp.sum(first.reshape(GROUPS, -1), axis=1) / members
    spread = jnp.sum(second.reshape(GROUPS, -1), axis=1) / members - group_mean * group_mean
    inverse = lax.rsqrt(spread + eps)
    grouped = values.reshape(frames, -1, GROUPS, channels // GROUPS)
    normed = (grouped - group_mean[:, None]) * inverse[:, None] * scaling.reshape(
        GROUPS, -1
    ) + offsets.reshape(GROUPS, -1)
    return jax.nn.silu(normed).reshape(values.shape)


def local(
    latents,
    frame_counts,
    clip_order,
    norm_scale,
    norm_offset,
    conv_weight,
    conv_bias,
    out_scale,
    out_offset,
):
    devices = lax.axis_size("tile")
    device = lax.axis_index("tile")
    frames, frame_rows, columns, channels = latents.shape
    tile_rows = frame_rows // NRB
    classes = devices // NRB
    per_dest = (frames + classes - 1) // classes
    worker_tiles = MEANF * NRB
    positions = jnp.arange(frame_counts.shape[0], dtype=jnp.int32)
    chosen = clip_order[:, None] == positions[None, :]
    ordered = jnp.sum(jnp.where(chosen, frame_counts[None, :], 0), axis=1)
    starts = (jnp.cumsum(ordered) - ordered) * NRB
    own_start = jnp.sum(jnp.where(clip_order == device, starts, 0))
    own_count = jnp.sum(jnp.where(positions == device, frame_counts, 0))

    active = normalize(latents.astype(jnp.float32), own_count, norm_scale, norm_offset).astype(
        jnp.bfloat16
    )
    padded = jnp.pad(active, ((2, 0), (1, 1), (1, 1), (0, 0)))
    unfolded = jnp.concatenate(
        [
            padded[frame_lag : frame_lag + frames, row_tap : row_tap + frame_rows, col_tap : col_tap + columns]
            for frame_lag in range(3)
            for row_tap in range(3)
            for col_tap in range(3)
        ],
        axis=-1,
    ).reshape(frames * frame_rows * columns, 27 * channels)
    conv = conv_bias + jnp.dot(
        unfolded, conv_weight.reshape(27 * channels, -1), preferred_element_type=jnp.float32
    )
    block_out = conv.astype(jnp.bfloat16).reshape(frames, frame_rows, columns, channels)
    per_group = channels // GROUPS
    value = block_out.astype(jnp.float32).reshape(frames, -1, channels)
    live_mask = (jnp.arange(frames) < own_count).astype(jnp.float32)[:, None]
    members = own_count.astype(jnp.float32) * (frame_rows * columns * per_group)
    frame_first = jnp.sum(value, axis=1)
    frame_second = jnp.sum(value * value, axis=1)
    first_sum = jnp.sum(jnp.sum(frame_first * live_mask, axis=0).reshape(GROUPS, per_group), axis=1)
    second_sum = jnp.sum(jnp.sum(frame_second * live_mask, axis=0).reshape(GROUPS, per_group), axis=1)
    clip_mean = first_sum / members
    clip_spread = second_sum / members - clip_mean * clip_mean
    clip_inverse = lax.rsqrt(clip_spread + eps)

    tiles = block_out.reshape(frames, NRB, tile_rows, columns, channels)
    tiles = jnp.pad(tiles, ((0, per_dest * classes - frames), (0, 0), (0, 0), (0, 0), (0, 0)))
    tiles = tiles.reshape(per_dest, classes, NRB, tile_rows, columns, channels)
    lag_of = (jnp.arange(classes, dtype=jnp.int32)[:, None] - (starts // NRB)[None, :] % classes) % classes
    pick = jnp.sum(jnp.where(clip_order[None, :] == device, lag_of, 0), axis=1)
    tiles = jnp.take(tiles, pick, axis=1)
    tiles = jnp.transpose(tiles, (1, 2, 0, 3, 4, 5)).reshape(
        devices, per_dest * tile_rows * columns, channels
    )
    stats = jnp.stack([clip_mean, clip_inverse], 0)
    stats = jnp.repeat(stats, per_group, axis=1)
    high = lax.reduce_precision(stats, exponent_bits=8, mantissa_bits=7)
    low = stats - high
    stat_rows = jnp.concatenate([high, low, jnp.zeros((4, channels), jnp.float32)], 0)
    stat_rows = jnp.broadcast_to(stat_rows.astype(jnp.bfloat16)[None], (devices, 8, channels))
    outgoing = jnp.concatenate([tiles, stat_rows], 1)
    received = lax.all_to_all(outgoing, "tile", split_axis=0, concat_axis=0, tiled=True)
    block_part = received[:, : per_dest * tile_rows * columns].reshape(
        devices * per_dest, tile_rows, columns, channels
    )
    stat_part = received[:, per_dest * tile_rows * columns :].astype(jnp.float32)
    src_mean = stat_part[:, 0] + stat_part[:, 2]
    src_inverse = stat_part[:, 1] + stat_part[:, 3]

    local_slot = jnp.arange(worker_tiles, dtype=jnp.int32)
    tile_id = local_slot * devices + device
    placed = jnp.sum((starts[None, :] <= tile_id[:, None]).astype(jnp.int32), axis=1) - 1
    at_place = placed[:, None] == positions[None, :]
    clip_id = jnp.sum(jnp.where(at_place, clip_order[None, :], 0), axis=1)
    within = tile_id - jnp.sum(jnp.where(at_place, starts[None, :], 0), axis=1)
    take_from = clip_id * per_dest + within // NRB // classes
    mine = jnp.take(block_part, take_from, axis=0)
    tile_mean = jnp.take(src_mean, clip_id, axis=0)
    tile_inverse = jnp.take(src_inverse, clip_id, axis=0)
    normed = (mine.astype(jnp.float32) - tile_mean[:, None, None, :]) * tile_inverse[
        :, None, None, :
    ] * out_scale + out_offset
    normed = jax.nn.silu(normed).astype(jnp.bfloat16)
    return (jnp.transpose(mine, (1, 0, 2, 3)), jnp.transpose(normed, (1, 0, 2, 3)))


def solution(mesh):
    in_specs = (
        P(("grp", "tile"), None, None, None),
        P("grp"),
        P("grp"),
        P(),
        P(),
        P(),
        P(),
        P(),
        P(),
    )
    out_specs = (P(None, ("grp", "tile"), None, None), P(None, ("grp", "tile"), None, None))
    return jax.shard_map(local, mesh=mesh, in_specs=in_specs, out_specs=out_specs, check_vma=False)
```

```python
import jax
import jax.numpy as jnp
from jax import lax
from jax.sharding import PartitionSpec as P

GROUPS = 32
MEANF = 4
NRB = 8


eps = 1e-06


def normalize(values, frame_count, scaling, offsets):
    frames = values.shape[0]
    channels = values.shape[-1]
    flat = values.reshape(frames, -1, channels)
    live_mask = (jnp.arange(frames) < frame_count).astype(jnp.float32)[:, None]
    members = frame_count.astype(jnp.float32) * flat.shape[1] * (channels // GROUPS)
    first = jnp.sum(jnp.sum(flat, axis=1) * live_mask, axis=0)
    second = jnp.sum(jnp.sum(flat * flat, axis=1) * live_mask, axis=0)
    group_mean = jnp.sum(first.reshape(GROUPS, -1), axis=1) / members
    spread = jnp.sum(second.reshape(GROUPS, -1), axis=1) / members - group_mean * group_mean
    inverse = lax.rsqrt(spread + eps)
    grouped = values.reshape(frames, -1, GROUPS, channels // GROUPS)
    normed = (grouped - group_mean[:, None]) * inverse[:, None] * scaling.reshape(
        GROUPS, -1
    ) + offsets.reshape(GROUPS, -1)
    return jax.nn.silu(normed).reshape(values.shape)


def local(
    latents,
    frame_counts,
    clip_order,
    norm_scale,
    norm_offset,
    conv_weight,
    conv_bias,
    out_scale,
    out_offset,
):
    devices = lax.axis_size("tile")
    device = lax.axis_index("tile")
    frames, frame_rows, columns, channels = latents.shape
    tile_rows = frame_rows // NRB
    classes = devices // NRB
    per_dest = (frames + classes - 1) // classes
    worker_tiles = MEANF * NRB
    positions = jnp.arange(frame_counts.shape[0], dtype=jnp.int32)
    chosen = clip_order[:, None] == positions[None, :]
    ordered = jnp.sum(jnp.where(chosen, frame_counts[None, :], 0), axis=1)
    starts = (jnp.cumsum(ordered) - ordered) * NRB
    own_count = jnp.sum(jnp.where(positions == device, frame_counts, 0))

    active = normalize(latents.astype(jnp.float32), own_count, norm_scale, norm_offset).astype(
        jnp.bfloat16
    )
    padded = jnp.pad(active, ((2, 0), (1, 1), (1, 1), (0, 0)))
    unfolded = jnp.concatenate(
        [
            padded[:, row_tap : row_tap + frame_rows, col_tap : col_tap + columns]
            for row_tap in range(3)
            for col_tap in range(3)
        ],
        axis=-1,
    ).reshape(frames + 2, frame_rows * columns, 9 * channels)
    kernel = conv_weight.reshape(3, 9 * channels, -1)
    conv = conv_bias + sum(
        jnp.dot(
            unfolded[frame_lag : frame_lag + frames].reshape(-1, 9 * channels),
            kernel[frame_lag],
            preferred_element_type=jnp.float32,
        )
        for frame_lag in range(3)
    ).reshape(frames, frame_rows, columns, -1)
    block_out = conv.astype(jnp.bfloat16)
    per_group = channels // GROUPS
    grouped = block_out.astype(jnp.float32).reshape(frames, frame_rows * columns, GROUPS, per_group)
    live_mask = (jnp.arange(frames) < own_count).astype(jnp.float32)[:, None, None, None]
    members = own_count.astype(jnp.float32) * (frame_rows * columns * per_group)
    first_sum = jnp.sum(grouped * live_mask, axis=(0, 1, 3))
    second_sum = jnp.sum(grouped * grouped * live_mask, axis=(0, 1, 3))
    clip_mean = first_sum / members
    clip_spread = second_sum / members - clip_mean * clip_mean
    clip_inverse = lax.rsqrt(clip_spread + eps)

    tiles = block_out.reshape(frames, NRB, tile_rows, columns, channels)
    tiles = jnp.pad(tiles, ((0, per_dest * classes - frames), (0, 0), (0, 0), (0, 0), (0, 0)))
    tiles = tiles.reshape(per_dest, classes, NRB, tile_rows, columns, channels)
    lag_of = (jnp.arange(classes, dtype=jnp.int32)[:, None] - (starts // NRB)[None, :] % classes) % classes
    pick = jnp.sum(jnp.where(clip_order[None, :] == device, lag_of, 0), axis=1)
    tiles = jnp.take(tiles, pick, axis=1)
    tiles = jnp.transpose(tiles, (1, 2, 0, 3, 4, 5)).reshape(
        devices, per_dest * tile_rows * columns, channels
    )
    stats = jnp.stack([clip_mean, clip_inverse], 0)
    stats = jnp.repeat(stats, per_group, axis=1)
    high = lax.reduce_precision(stats, exponent_bits=8, mantissa_bits=7)
    low = stats - high
    stat_rows = jnp.concatenate([high, low, jnp.zeros((4, channels), jnp.float32)], 0)
    stat_rows = jnp.broadcast_to(stat_rows.astype(jnp.bfloat16)[None], (devices, 8, channels))
    outgoing = jnp.concatenate([tiles, stat_rows], 1)
    received = lax.all_to_all(outgoing, "tile", split_axis=0, concat_axis=0, tiled=True)
    block_part = received[:, : per_dest * tile_rows * columns].reshape(
        devices * per_dest, tile_rows, columns, channels
    )
    stat_part = received[:, per_dest * tile_rows * columns :].astype(jnp.float32)
    src_mean = stat_part[:, 0] + stat_part[:, 2]
    src_inverse = stat_part[:, 1] + stat_part[:, 3]

    local_slot = jnp.arange(worker_tiles, dtype=jnp.int32)
    tile_id = local_slot * devices + device
    placed = jnp.sum((starts[None, :] <= tile_id[:, None]).astype(jnp.int32), axis=1) - 1
    at_place = placed[:, None] == positions[None, :]
    clip_id = jnp.sum(jnp.where(at_place, clip_order[None, :], 0), axis=1)
    within = tile_id - jnp.sum(jnp.where(at_place, starts[None, :], 0), axis=1)
    take_from = clip_id * per_dest + within // NRB // classes
    mine = jnp.take(block_part, take_from, axis=0)
    tile_mean = jnp.take(src_mean, clip_id, axis=0)
    tile_inverse = jnp.take(src_inverse, clip_id, axis=0)
    normed = (mine.astype(jnp.float32) - tile_mean[:, None, None, :]) * tile_inverse[
        :, None, None, :
    ] * out_scale + out_offset
    normed = jax.nn.silu(normed).astype(jnp.bfloat16)
    return (jnp.transpose(mine, (1, 0, 2, 3)), jnp.transpose(normed, (1, 0, 2, 3)))


def solution(mesh):
    in_specs = (
        P(("grp", "tile"), None, None, None),
        P("grp"),
        P("grp"),
        P(),
        P(),
        P(),
        P(),
        P(),
        P(),
    )
    out_specs = (P(None, ("grp", "tile"), None, None), P(None, ("grp", "tile"), None, None))
    return jax.shard_map(local, mesh=mesh, in_specs=in_specs, out_specs=out_specs, check_vma=False)
```

```python
import jax
import jax.numpy as jnp
from jax import lax
from jax.sharding import PartitionSpec as P

GROUPS = 32
MEANF = 4
NRB = 8


eps = 1e-06


def normalize(values, frame_count, scaling, offsets):
    frames = values.shape[0]
    channels = values.shape[-1]
    flat = values.reshape(frames, -1, channels)
    live_mask = (jnp.arange(frames) < frame_count).astype(jnp.float32)[:, None]
    members = frame_count.astype(jnp.float32) * flat.shape[1] * (channels // GROUPS)
    first = jnp.sum(jnp.sum(flat, axis=1) * live_mask, axis=0)
    second = jnp.sum(jnp.sum(flat * flat, axis=1) * live_mask, axis=0)
    group_mean = jnp.sum(first.reshape(GROUPS, -1), axis=1) / members
    spread = jnp.sum(second.reshape(GROUPS, -1), axis=1) / members - group_mean * group_mean
    inverse = lax.rsqrt(spread + eps)
    grouped = values.reshape(frames, -1, GROUPS, channels // GROUPS)
    normed = (grouped - group_mean[:, None]) * inverse[:, None] * scaling.reshape(
        GROUPS, -1
    ) + offsets.reshape(GROUPS, -1)
    return jax.nn.silu(normed).reshape(values.shape)


def local(
    latents,
    frame_counts,
    clip_order,
    norm_scale,
    norm_offset,
    conv_weight,
    conv_bias,
    out_scale,
    out_offset,
):
    devices = lax.axis_size("tile")
    device = lax.axis_index("tile")
    frames, frame_rows, columns, channels = latents.shape
    tile_rows = frame_rows // NRB
    classes = devices // NRB
    per_dest = (frames + classes - 1) // classes
    worker_tiles = MEANF * NRB
    positions = jnp.arange(frame_counts.shape[0], dtype=jnp.int32)
    chosen = clip_order[:, None] == positions[None, :]
    ordered = jnp.sum(jnp.where(chosen, frame_counts[None, :], 0), axis=1)
    starts = (jnp.cumsum(ordered) - ordered) * NRB
    own_count = jnp.sum(jnp.where(positions == device, frame_counts, 0))

    active = normalize(latents.astype(jnp.float32), own_count, norm_scale, norm_offset).astype(
        jnp.bfloat16
    )
    padded = jnp.pad(active, ((2, 0), (1, 1), (1, 1), (0, 0)))
    unfolded = jnp.concatenate(
        [
            padded[:, row_tap : row_tap + frame_rows, col_tap : col_tap + columns]
            for row_tap in range(3)
            for col_tap in range(3)
        ],
        axis=-1,
    ).reshape(frames + 2, frame_rows * columns, 9 * channels)
    kernel = conv_weight.reshape(3, 9 * channels, -1)
    spread_out = [
        jnp.dot(
            unfolded.reshape(-1, 9 * channels), kernel[frame_lag], preferred_element_type=jnp.float32
        ).reshape(frames + 2, frame_rows * columns, -1)
        for frame_lag in range(3)
    ]
    conv = conv_bias + sum(
        spread_out[frame_lag][frame_lag : frame_lag + frames] for frame_lag in range(3)
    )
    conv = conv.reshape(frames, frame_rows, columns, -1)
    block_out = conv.astype(jnp.bfloat16)
    per_group = channels // GROUPS
    grouped = block_out.astype(jnp.float32).reshape(frames, frame_rows * columns, GROUPS, per_group)
    live_mask = (jnp.arange(frames) < own_count).astype(jnp.float32)[:, None, None, None]
    members = own_count.astype(jnp.float32) * (frame_rows * columns * per_group)
    first_sum = jnp.sum(grouped * live_mask, axis=(0, 1, 3))
    second_sum = jnp.sum(grouped * grouped * live_mask, axis=(0, 1, 3))
    clip_mean = first_sum / members
    clip_spread = second_sum / members - clip_mean * clip_mean
    clip_inverse = lax.rsqrt(clip_spread + eps)

    tiles = block_out.reshape(frames, NRB, tile_rows, columns, channels)
    tiles = jnp.pad(tiles, ((0, per_dest * classes - frames), (0, 0), (0, 0), (0, 0), (0, 0)))
    tiles = tiles.reshape(per_dest, classes, NRB, tile_rows, columns, channels)
    lag_of = (jnp.arange(classes, dtype=jnp.int32)[:, None] - (starts // NRB)[None, :] % classes) % classes
    pick = jnp.sum(jnp.where(clip_order[None, :] == device, lag_of, 0), axis=1)
    tiles = jnp.take(tiles, pick, axis=1)
    tiles = jnp.transpose(tiles, (1, 2, 3, 0, 4, 5)).reshape(
        devices, tile_rows * per_dest * columns, channels
    )
    stats = jnp.stack([clip_mean, clip_inverse], 0)
    stats = jnp.repeat(stats, per_group, axis=1)
    high = lax.reduce_precision(stats, exponent_bits=8, mantissa_bits=7)
    low = stats - high
    stat_rows = jnp.concatenate([high, low, jnp.zeros((4, channels), jnp.float32)], 0)
    stat_rows = jnp.broadcast_to(stat_rows.astype(jnp.bfloat16)[None], (devices, 8, channels))
    outgoing = jnp.concatenate([tiles, stat_rows], 1)
    received = lax.all_to_all(outgoing, "tile", split_axis=0, concat_axis=0, tiled=True)
    block_part = received[:, : per_dest * tile_rows * columns].reshape(
        devices, tile_rows, per_dest, columns, channels
    )
    stat_part = received[:, per_dest * tile_rows * columns :].astype(jnp.float32)
    src_mean = stat_part[:, 0] + stat_part[:, 2]
    src_inverse = stat_part[:, 1] + stat_part[:, 3]
    normed_part = (block_part.astype(jnp.float32) - src_mean[:, None, None, None, :]) * src_inverse[
        :, None, None, None, :
    ] * out_scale + out_offset
    normed_part = jax.nn.silu(normed_part).astype(jnp.bfloat16)

    local_slot = jnp.arange(worker_tiles, dtype=jnp.int32)
    tile_id = local_slot * devices + device
    placed = jnp.sum((starts[None, :] <= tile_id[:, None]).astype(jnp.int32), axis=1) - 1
    at_place = placed[:, None] == positions[None, :]
    clip_id = jnp.sum(jnp.where(at_place, clip_order[None, :], 0), axis=1)
    within = tile_id - jnp.sum(jnp.where(at_place, starts[None, :], 0), axis=1)
    row_of = jnp.arange(tile_rows, dtype=jnp.int32)[:, None]
    take_from = (clip_id[None, :] * tile_rows + row_of) * per_dest + (within // NRB // classes)[None, :]
    rows_all = devices * tile_rows * per_dest
    block_mine = jnp.take(block_part.reshape(rows_all, columns, channels), take_from, axis=0)
    normed_mine = jnp.take(normed_part.reshape(rows_all, columns, channels), take_from, axis=0)
    return (block_mine, normed_mine)


def solution(mesh):
    in_specs = (
        P(("grp", "tile"), None, None, None),
        P("grp"),
        P("grp"),
        P(),
        P(),
        P(),
        P(),
        P(),
        P(),
    )
    out_specs = (P(None, ("grp", "tile"), None, None), P(None, ("grp", "tile"), None, None))
    return jax.shard_map(local, mesh=mesh, in_specs=in_specs, out_specs=out_specs, check_vma=False)
```

```python
import jax
import jax.numpy as jnp
from jax import lax
from jax.sharding import PartitionSpec as P

GROUPS = 32
MEANF = 4
NRB = 8


eps = 1e-06


def normalize(values, frame_count, scaling, offsets):
    frames = values.shape[0]
    channels = values.shape[-1]
    flat = values.reshape(frames, -1, channels)
    live_mask = (jnp.arange(frames) < frame_count).astype(jnp.float32)[:, None]
    members = frame_count.astype(jnp.float32) * flat.shape[1] * (channels // GROUPS)
    first = jnp.sum(jnp.sum(flat, axis=1) * live_mask, axis=0)
    second = jnp.sum(jnp.sum(flat * flat, axis=1) * live_mask, axis=0)
    group_mean = jnp.sum(first.reshape(GROUPS, -1), axis=1) / members
    spread = jnp.sum(second.reshape(GROUPS, -1), axis=1) / members - group_mean * group_mean
    inverse = lax.rsqrt(spread + eps)
    grouped = values.reshape(frames, -1, GROUPS, channels // GROUPS)
    normed = (grouped - group_mean[:, None]) * inverse[:, None] * scaling.reshape(
        GROUPS, -1
    ) + offsets.reshape(GROUPS, -1)
    return jax.nn.silu(normed).reshape(values.shape)


def local(
    latents,
    frame_counts,
    clip_order,
    norm_scale,
    norm_offset,
    conv_weight,
    conv_bias,
    out_scale,
    out_offset,
):
    devices = lax.axis_size("tile")
    device = lax.axis_index("tile")
    frames, frame_rows, columns, channels = latents.shape
    tile_rows = frame_rows // NRB
    classes = devices // NRB
    per_dest = (frames + classes - 1) // classes
    worker_tiles = MEANF * NRB
    meta = lax.optimization_barrier(jnp.stack([frame_counts, clip_order], 0))
    frame_counts, clip_order = meta[0], meta[1]
    positions = jnp.arange(frame_counts.shape[0], dtype=jnp.int32)
    chosen = clip_order[:, None] == positions[None, :]
    ordered = jnp.sum(jnp.where(chosen, frame_counts[None, :], 0), axis=1)
    starts = (jnp.cumsum(ordered) - ordered) * NRB
    own_count = jnp.sum(jnp.where(positions == device, frame_counts, 0))

    active = normalize(latents.astype(jnp.float32), own_count, norm_scale, norm_offset).astype(
        jnp.bfloat16
    )
    padded = jnp.pad(active, ((2, 0), (1, 1), (1, 1), (0, 0)))
    unfolded = jnp.concatenate(
        [
            padded[:, row_tap : row_tap + frame_rows, col_tap : col_tap + columns]
            for row_tap in range(3)
            for col_tap in range(3)
        ],
        axis=-1,
    ).reshape(frames + 2, frame_rows * columns, 9 * channels)
    kernel = conv_weight.reshape(3, 9 * channels, -1)
    spread_out = [
        jnp.dot(
            unfolded.reshape(-1, 9 * channels), kernel[frame_lag], preferred_element_type=jnp.float32
        ).reshape(frames + 2, frame_rows * columns, -1)
        for frame_lag in range(3)
    ]
    conv = conv_bias + sum(
        spread_out[frame_lag][frame_lag : frame_lag + frames] for frame_lag in range(3)
    )
    conv = conv.reshape(frames, frame_rows, columns, -1)
    block_out = conv.astype(jnp.bfloat16)
    per_group = channels // GROUPS
    grouped = block_out.astype(jnp.float32).reshape(frames, frame_rows * columns, GROUPS, per_group)
    live_mask = (jnp.arange(frames) < own_count).astype(jnp.float32)[:, None, None, None]
    members = own_count.astype(jnp.float32) * (frame_rows * columns * per_group)
    first_sum = jnp.sum(grouped * live_mask, axis=(0, 1, 3))
    second_sum = jnp.sum(grouped * grouped * live_mask, axis=(0, 1, 3))
    clip_mean = first_sum / members
    clip_spread = second_sum / members - clip_mean * clip_mean
    clip_inverse = lax.rsqrt(clip_spread + eps)

    tiles = block_out.reshape(frames, NRB, tile_rows, columns, channels)
    tiles = jnp.pad(tiles, ((0, per_dest * classes - frames), (0, 0), (0, 0), (0, 0), (0, 0)))
    tiles = tiles.reshape(per_dest, classes, NRB, tile_rows, columns, channels)
    lag_of = (jnp.arange(classes, dtype=jnp.int32)[:, None] - (starts // NRB)[None, :] % classes) % classes
    pick = jnp.sum(jnp.where(clip_order[None, :] == device, lag_of, 0), axis=1)
    tiles = jnp.take(tiles, pick, axis=1)
    tiles = jnp.transpose(tiles, (1, 2, 3, 0, 4, 5)).reshape(
        devices, tile_rows * per_dest * columns, channels
    )
    stats = jnp.stack([clip_mean, clip_inverse], 0)
    stats = jnp.repeat(stats, per_group, axis=1)
    high = lax.reduce_precision(stats, exponent_bits=8, mantissa_bits=7)
    low = stats - high
    stat_rows = jnp.concatenate([high, low, jnp.zeros((4, channels), jnp.float32)], 0)
    stat_rows = jnp.broadcast_to(stat_rows.astype(jnp.bfloat16)[None], (devices, 8, channels))
    outgoing = jnp.concatenate([tiles, stat_rows], 1)
    received = lax.all_to_all(outgoing, "tile", split_axis=0, concat_axis=0, tiled=True)
    block_part = received[:, : per_dest * tile_rows * columns].reshape(
        devices, tile_rows, per_dest, columns, channels
    )
    stat_part = received[:, per_dest * tile_rows * columns :].astype(jnp.float32)
    src_mean = stat_part[:, 0] + stat_part[:, 2]
    src_inverse = stat_part[:, 1] + stat_part[:, 3]
    normed_part = (block_part.astype(jnp.float32) - src_mean[:, None, None, None, :]) * src_inverse[
        :, None, None, None, :
    ] * out_scale + out_offset
    normed_part = jax.nn.silu(normed_part).astype(jnp.bfloat16)

    local_slot = jnp.arange(worker_tiles, dtype=jnp.int32)
    tile_id = local_slot * devices + device
    placed = jnp.sum((starts[None, :] <= tile_id[:, None]).astype(jnp.int32), axis=1) - 1
    at_place = placed[:, None] == positions[None, :]
    clip_id = jnp.sum(jnp.where(at_place, clip_order[None, :], 0), axis=1)
    within = tile_id - jnp.sum(jnp.where(at_place, starts[None, :], 0), axis=1)
    row_of = jnp.arange(tile_rows, dtype=jnp.int32)[:, None]
    take_from = (clip_id[None, :] * tile_rows + row_of) * per_dest + (within // NRB // classes)[None, :]
    rows_all = devices * tile_rows * per_dest
    block_mine = jnp.take(block_part.reshape(rows_all, columns, channels), take_from, axis=0)
    normed_mine = jnp.take(normed_part.reshape(rows_all, columns, channels), take_from, axis=0)
    return (block_mine, normed_mine)


def solution(mesh):
    in_specs = (
        P(("grp", "tile"), None, None, None),
        P("grp"),
        P("grp"),
        P(),
        P(),
        P(),
        P(),
        P(),
        P(),
    )
    out_specs = (P(None, ("grp", "tile"), None, None), P(None, ("grp", "tile"), None, None))
    return jax.shard_map(local, mesh=mesh, in_specs=in_specs, out_specs=out_specs, check_vma=False)
```

```python
import jax
import jax.numpy as jnp
from jax import lax
from jax.sharding import PartitionSpec as P

GROUPS = 32
MEANF = 4
NRB = 8


eps = 1e-06


def normalize(values, frame_count, scaling, offsets):
    frames = values.shape[0]
    channels = values.shape[-1]
    flat = values.reshape(frames, -1, channels)
    live_mask = (jnp.arange(frames) < frame_count).astype(jnp.float32)[:, None]
    members = frame_count.astype(jnp.float32) * flat.shape[1] * (channels // GROUPS)
    first = jnp.sum(jnp.sum(flat, axis=1) * live_mask, axis=0)
    second = jnp.sum(jnp.sum(flat * flat, axis=1) * live_mask, axis=0)
    group_mean = jnp.sum(first.reshape(GROUPS, -1), axis=1) / members
    spread = jnp.sum(second.reshape(GROUPS, -1), axis=1) / members - group_mean * group_mean
    inverse = lax.rsqrt(spread + eps)
    grouped = values.reshape(frames, -1, GROUPS, channels // GROUPS)
    normed = (grouped - group_mean[:, None]) * inverse[:, None] * scaling.reshape(
        GROUPS, -1
    ) + offsets.reshape(GROUPS, -1)
    return jax.nn.silu(normed).reshape(values.shape)


def local(
    latents,
    frame_counts,
    clip_order,
    norm_scale,
    norm_offset,
    conv_weight,
    conv_bias,
    out_scale,
    out_offset,
):
    devices = lax.axis_size("tile")
    device = lax.axis_index("tile")
    frames, frame_rows, columns, channels = latents.shape
    tile_rows = frame_rows // NRB
    classes = devices // NRB
    per_dest = (frames + classes - 1) // classes
    worker_tiles = MEANF * NRB
    meta = lax.optimization_barrier(jnp.stack([frame_counts, clip_order], 0))
    frame_counts, clip_order = meta[0], meta[1]
    positions = jnp.arange(frame_counts.shape[0], dtype=jnp.int32)
    chosen = clip_order[:, None] == positions[None, :]
    ordered = jnp.sum(jnp.where(chosen, frame_counts[None, :], 0), axis=1)
    starts = (jnp.cumsum(ordered) - ordered) * NRB
    own_count = jnp.sum(jnp.where(positions == device, frame_counts, 0))

    active = normalize(latents.astype(jnp.float32), own_count, norm_scale, norm_offset).astype(
        jnp.bfloat16
    )
    padded = jnp.pad(active, ((2, 0), (1, 1), (1, 1), (0, 0)))
    unfolded = jnp.concatenate(
        [
            padded[:, row_tap : row_tap + frame_rows, col_tap : col_tap + columns]
            for row_tap in range(3)
            for col_tap in range(3)
        ],
        axis=-1,
    ).reshape(frames + 2, frame_rows * columns, 9 * channels)
    kernel = conv_weight.reshape(3, 9 * channels, -1)
    spread_out = [
        jnp.dot(
            unfolded.reshape(-1, 9 * channels), kernel[frame_lag], preferred_element_type=jnp.float32
        ).reshape(frames + 2, frame_rows * columns, -1)
        for frame_lag in range(3)
    ]
    conv = conv_bias + sum(
        spread_out[frame_lag][frame_lag : frame_lag + frames] for frame_lag in range(3)
    )
    conv = conv.reshape(frames, frame_rows, columns, -1)
    block_out = conv.astype(jnp.bfloat16)
    per_group = channels // GROUPS
    grouped = block_out.astype(jnp.float32).reshape(frames, frame_rows * columns, GROUPS, per_group)
    live_mask = (jnp.arange(frames) < own_count).astype(jnp.float32)[:, None, None, None]
    members = own_count.astype(jnp.float32) * (frame_rows * columns * per_group)
    first_sum = jnp.sum(grouped * live_mask, axis=(0, 1, 3))
    second_sum = jnp.sum(grouped * grouped * live_mask, axis=(0, 1, 3))
    clip_mean = first_sum / members
    clip_spread = second_sum / members - clip_mean * clip_mean
    clip_inverse = lax.rsqrt(clip_spread + eps)

    tiles = block_out.reshape(frames, NRB, tile_rows, columns, channels)
    tiles = jnp.pad(tiles, ((0, per_dest * classes - frames), (0, 0), (0, 0), (0, 0), (0, 0)))
    tiles = tiles.reshape(per_dest, classes, NRB, tile_rows, columns, channels)
    lag_of = (jnp.arange(classes, dtype=jnp.int32)[:, None] - (starts // NRB)[None, :] % classes) % classes
    pick = jnp.sum(jnp.where(clip_order[None, :] == device, lag_of, 0), axis=1)
    tiles = jnp.take(tiles, pick, axis=1, mode="clip")
    tiles = jnp.transpose(tiles, (1, 2, 3, 0, 4, 5)).reshape(
        devices, tile_rows * per_dest * columns, channels
    )
    stats = jnp.stack([clip_mean, clip_inverse], 0)
    stats = jnp.repeat(stats, per_group, axis=1)
    high = lax.reduce_precision(stats, exponent_bits=8, mantissa_bits=7)
    low = stats - high
    stat_rows = jnp.concatenate([high, low, jnp.zeros((4, channels), jnp.float32)], 0)
    stat_rows = jnp.broadcast_to(stat_rows.astype(jnp.bfloat16)[None], (devices, 8, channels))
    outgoing = jnp.concatenate([tiles, stat_rows], 1)
    received = lax.all_to_all(outgoing, "tile", split_axis=0, concat_axis=0, tiled=True)
    block_part = received[:, : per_dest * tile_rows * columns].reshape(
        devices, tile_rows, per_dest, columns, channels
    )
    stat_part = received[:, per_dest * tile_rows * columns :].astype(jnp.float32)
    src_mean = stat_part[:, 0] + stat_part[:, 2]
    src_inverse = stat_part[:, 1] + stat_part[:, 3]
    normed_part = (block_part.astype(jnp.float32) - src_mean[:, None, None, None, :]) * src_inverse[
        :, None, None, None, :
    ] * out_scale + out_offset
    normed_part = jax.nn.silu(normed_part).astype(jnp.bfloat16)

    local_slot = jnp.arange(worker_tiles, dtype=jnp.int32)
    tile_id = local_slot * devices + device
    placed = jnp.sum((starts[None, :] <= tile_id[:, None]).astype(jnp.int32), axis=1) - 1
    at_place = placed[:, None] == positions[None, :]
    clip_id = jnp.sum(jnp.where(at_place, clip_order[None, :], 0), axis=1)
    within = tile_id - jnp.sum(jnp.where(at_place, starts[None, :], 0), axis=1)
    row_of = jnp.arange(tile_rows, dtype=jnp.int32)[:, None]
    take_from = (clip_id[None, :] * tile_rows + row_of) * per_dest + (within // NRB // classes)[None, :]
    rows_all = devices * tile_rows * per_dest
    block_mine = jnp.take(block_part.reshape(rows_all, columns, channels), take_from, axis=0, mode="clip")
    normed_mine = jnp.take(normed_part.reshape(rows_all, columns, channels), take_from, axis=0, mode="clip")
    return (block_mine, normed_mine)


def solution(mesh):
    in_specs = (
        P(("grp", "tile"), None, None, None),
        P("grp"),
        P("grp"),
        P(),
        P(),
        P(),
        P(),
        P(),
        P(),
    )
    out_specs = (P(None, ("grp", "tile"), None, None), P(None, ("grp", "tile"), None, None))
    return jax.shard_map(local, mesh=mesh, in_specs=in_specs, out_specs=out_specs, check_vma=False)
```

```python
import functools

import jax
import jax.numpy as jnp
from jax import lax
from jax.experimental import pallas as pl
from jax.experimental.pallas import tpu as pltpu
from jax.sharding import PartitionSpec as P

GROUPS = 32
MEANF = 4
NRB = 8


eps = 1e-06


def normalize(values, frame_count, scaling, offsets):
    frames = values.shape[0]
    channels = values.shape[-1]
    flat = values.reshape(frames, -1, channels)
    live_mask = (jnp.arange(frames) < frame_count).astype(jnp.float32)[:, None]
    members = frame_count.astype(jnp.float32) * flat.shape[1] * (channels // GROUPS)
    first = jnp.sum(jnp.sum(flat, axis=1) * live_mask, axis=0)
    second = jnp.sum(jnp.sum(flat * flat, axis=1) * live_mask, axis=0)
    group_mean = jnp.sum(first.reshape(GROUPS, -1), axis=1) / members
    spread = jnp.sum(second.reshape(GROUPS, -1), axis=1) / members - group_mean * group_mean
    inverse = lax.rsqrt(spread + eps)
    grouped = values.reshape(frames, -1, GROUPS, channels // GROUPS)
    normed = (grouped - group_mean[:, None]) * inverse[:, None] * scaling.reshape(
        GROUPS, -1
    ) + offsets.reshape(GROUPS, -1)
    return jax.nn.silu(normed).reshape(values.shape)


def conv_body(act_ref, w_hbm, b_ref, o_ref, s1_ref, s2_ref, w_vmem, unfolded, sems, *, frame_rows, columns):
    positions = frame_rows * columns
    rows, channels = act_ref.shape
    frames = rows // positions
    copies = [pltpu.make_async_copy(w_hbm.at[lag], w_vmem.at[lag], sems.at[lag]) for lag in range(3)]
    for copy in copies:
        copy.start()
    values = act_ref[...].astype(jnp.float32)
    flat = lax.broadcasted_iota(jnp.int32, (rows, channels), 0)
    column = flat % columns
    row = (flat // columns) % frame_rows
    unfolded[0 : 2 * positions, :] = jnp.zeros((2 * positions, 9 * channels), unfolded.dtype)
    for row_tap in range(3):
        for col_tap in range(3):
            offset = (row_tap - 1) * columns + (col_tap - 1)
            moved = values if offset == 0 else pltpu.roll(values, (-offset) % rows, 0)
            keep = (
                (row + row_tap - 1 >= 0)
                & (row + row_tap - 1 < frame_rows)
                & (column + col_tap - 1 >= 0)
                & (column + col_tap - 1 < columns)
            )
            tap = row_tap * 3 + col_tap
            unfolded[2 * positions :, tap * channels : (tap + 1) * channels] = jnp.where(
                keep, moved, 0.0
            ).astype(unfolded.dtype)
    acc = jnp.broadcast_to(b_ref[...], (rows, o_ref.shape[-1]))
    for lag in range(3):
        copies[lag].wait()
        acc = acc + jnp.dot(
            unfolded[lag * positions : lag * positions + rows, :],
            w_vmem[lag],
            preferred_element_type=jnp.float32,
        )
    out = acc.astype(o_ref.dtype)
    o_ref[...] = out
    value = out.astype(jnp.float32).reshape(frames, positions, -1)
    s1_ref[...] = jnp.sum(value, axis=1, keepdims=True)
    s2_ref[...] = jnp.sum(value * value, axis=1, keepdims=True)


def conv_call(active, kernel, bias):
    frames, frame_rows, columns, channels = active.shape
    positions = frame_rows * columns
    out_channels = kernel.shape[-1]
    vmem = pl.BlockSpec(memory_space=pltpu.VMEM)
    return pl.pallas_call(
        functools.partial(conv_body, frame_rows=frame_rows, columns=columns),
        out_shape=(
            jax.ShapeDtypeStruct((frames * positions, out_channels), jnp.bfloat16),
            jax.ShapeDtypeStruct((frames, 1, out_channels), jnp.float32),
            jax.ShapeDtypeStruct((frames, 1, out_channels), jnp.float32),
        ),
        in_specs=[vmem, pl.BlockSpec(memory_space=pltpu.HBM), vmem],
        out_specs=(vmem, vmem, vmem),
        scratch_shapes=[
            pltpu.VMEM(kernel.shape, kernel.dtype),
            pltpu.VMEM(((frames + 2) * positions, 9 * channels), jnp.bfloat16),
            pltpu.SemaphoreType.DMA((3,)),
        ],
        compiler_params=pltpu.CompilerParams(vmem_limit_bytes=48 * 1024 * 1024),
        cost_estimate=pl.CostEstimate(
            flops=2 * frames * positions * 3 * kernel.shape[1] * out_channels,
            transcendentals=0,
            bytes_accessed=active.size * 2 + kernel.size * 2 + frames * positions * out_channels * 2,
        ),
    )(active.reshape(frames * positions, channels), kernel, bias.reshape(1, out_channels))


def local(
    latents,
    frame_counts,
    clip_order,
    norm_scale,
    norm_offset,
    conv_weight,
    conv_bias,
    out_scale,
    out_offset,
):
    devices = lax.axis_size("tile")
    device = lax.axis_index("tile")
    frames, frame_rows, columns, channels = latents.shape
    tile_rows = frame_rows // NRB
    classes = devices // NRB
    per_dest = (frames + classes - 1) // classes
    worker_tiles = MEANF * NRB
    meta = lax.optimization_barrier(jnp.stack([frame_counts, clip_order], 0))
    frame_counts, clip_order = meta[0], meta[1]
    positions = jnp.arange(frame_counts.shape[0], dtype=jnp.int32)
    chosen = clip_order[:, None] == positions[None, :]
    ordered = jnp.sum(jnp.where(chosen, frame_counts[None, :], 0), axis=1)
    starts = (jnp.cumsum(ordered) - ordered) * NRB
    own_count = jnp.sum(jnp.where(positions == device, frame_counts, 0))

    active = normalize(latents.astype(jnp.float32), own_count, norm_scale, norm_offset).astype(
        jnp.bfloat16
    )
    conv_flat, frame_first, frame_second = conv_call(
        active, conv_weight.reshape(3, 9 * channels, -1), conv_bias
    )
    block_out = conv_flat.reshape(frames, frame_rows, columns, channels)
    per_group = channels // GROUPS
    live_mask = (jnp.arange(frames) < own_count).astype(jnp.float32)[:, None]
    members = own_count.astype(jnp.float32) * (frame_rows * columns * per_group)
    first_sum = jnp.sum(jnp.sum(frame_first[:, 0] * live_mask, axis=0).reshape(GROUPS, per_group), axis=1)
    second_sum = jnp.sum(jnp.sum(frame_second[:, 0] * live_mask, axis=0).reshape(GROUPS, per_group), axis=1)
    clip_mean = first_sum / members
    clip_spread = second_sum / members - clip_mean * clip_mean
    clip_inverse = lax.rsqrt(clip_spread + eps)

    tiles = block_out.reshape(frames, NRB, tile_rows, columns, channels)
    tiles = jnp.pad(tiles, ((0, per_dest * classes - frames), (0, 0), (0, 0), (0, 0), (0, 0)))
    tiles = tiles.reshape(per_dest, classes, NRB, tile_rows, columns, channels)
    lag_of = (jnp.arange(classes, dtype=jnp.int32)[:, None] - (starts // NRB)[None, :] % classes) % classes
    pick = jnp.sum(jnp.where(clip_order[None, :] == device, lag_of, 0), axis=1)
    tiles = jnp.take(tiles, pick, axis=1, mode="clip")
    tiles = jnp.transpose(tiles, (1, 2, 3, 0, 4, 5)).reshape(
        devices, tile_rows * per_dest * columns, channels
    )
    stats = jnp.stack([clip_mean, clip_inverse], 0)
    stats = jnp.repeat(stats, per_group, axis=1)
    high = lax.reduce_precision(stats, exponent_bits=8, mantissa_bits=7)
    low = stats - high
    stat_rows = jnp.concatenate([high, low, jnp.zeros((4, channels), jnp.float32)], 0)
    stat_rows = jnp.broadcast_to(stat_rows.astype(jnp.bfloat16)[None], (devices, 8, channels))
    outgoing = jnp.concatenate([tiles, stat_rows], 1)
    received = lax.all_to_all(outgoing, "tile", split_axis=0, concat_axis=0, tiled=True)
    block_part = received[:, : per_dest * tile_rows * columns].reshape(
        devices, tile_rows, per_dest, columns, channels
    )
    stat_part = received[:, per_dest * tile_rows * columns :].astype(jnp.float32)
    src_mean = stat_part[:, 0] + stat_part[:, 2]
    src_inverse = stat_part[:, 1] + stat_part[:, 3]
    normed_part = (block_part.astype(jnp.float32) - src_mean[:, None, None, None, :]) * src_inverse[
        :, None, None, None, :
    ] * out_scale + out_offset
    normed_part = jax.nn.silu(normed_part).astype(jnp.bfloat16)

    local_slot = jnp.arange(worker_tiles, dtype=jnp.int32)
    tile_id = local_slot * devices + device
    placed = jnp.sum((starts[None, :] <= tile_id[:, None]).astype(jnp.int32), axis=1) - 1
    at_place = placed[:, None] == positions[None, :]
    clip_id = jnp.sum(jnp.where(at_place, clip_order[None, :], 0), axis=1)
    within = tile_id - jnp.sum(jnp.where(at_place, starts[None, :], 0), axis=1)
    row_of = jnp.arange(tile_rows, dtype=jnp.int32)[:, None]
    take_from = (clip_id[None, :] * tile_rows + row_of) * per_dest + (within // NRB // classes)[None, :]
    rows_all = devices * tile_rows * per_dest
    block_mine = jnp.take(block_part.reshape(rows_all, columns, channels), take_from, axis=0, mode="clip")
    normed_mine = jnp.take(normed_part.reshape(rows_all, columns, channels), take_from, axis=0, mode="clip")
    return (block_mine, normed_mine)


def solution(mesh):
    in_specs = (
        P(("grp", "tile"), None, None, None),
        P("grp"),
        P("grp"),
        P(),
        P(),
        P(),
        P(),
        P(),
        P(),
    )
    out_specs = (P(None, ("grp", "tile"), None, None), P(None, ("grp", "tile"), None, None))
    return jax.shard_map(local, mesh=mesh, in_specs=in_specs, out_specs=out_specs, check_vma=False)
```

```python
import jax
import jax.numpy as jnp
from jax import lax
from jax.sharding import PartitionSpec as P

GROUPS = 32
MEANF = 4
NRB = 8


eps = 1e-06


def normalize(values, frame_count, scaling, offsets):
    frames = values.shape[0]
    channels = values.shape[-1]
    flat = values.reshape(frames, -1, channels)
    live_mask = (jnp.arange(frames) < frame_count).astype(jnp.float32)[:, None]
    members = frame_count.astype(jnp.float32) * flat.shape[1] * (channels // GROUPS)
    first = jnp.sum(jnp.sum(flat, axis=1) * live_mask, axis=0)
    second = jnp.sum(jnp.sum(flat * flat, axis=1) * live_mask, axis=0)
    group_mean = jnp.sum(first.reshape(GROUPS, -1), axis=1) / members
    spread = jnp.sum(second.reshape(GROUPS, -1), axis=1) / members - group_mean * group_mean
    inverse = lax.rsqrt(spread + eps)
    grouped = values.reshape(frames, -1, GROUPS, channels // GROUPS)
    normed = (grouped - group_mean[:, None]) * inverse[:, None] * scaling.reshape(
        GROUPS, -1
    ) + offsets.reshape(GROUPS, -1)
    return jax.nn.silu(normed).reshape(values.shape)


def local(
    latents,
    frame_counts,
    clip_order,
    norm_scale,
    norm_offset,
    conv_weight,
    conv_bias,
    out_scale,
    out_offset,
):
    devices = lax.axis_size("tile")
    device = lax.axis_index("tile")
    frames, frame_rows, columns, channels = latents.shape
    tile_rows = frame_rows // NRB
    classes = devices // NRB
    per_dest = (frames + classes - 1) // classes
    worker_tiles = MEANF * NRB
    meta = lax.optimization_barrier(jnp.stack([frame_counts, clip_order], 0))
    frame_counts, clip_order = meta[0], meta[1]
    positions = jnp.arange(frame_counts.shape[0], dtype=jnp.int32)
    chosen = clip_order[:, None] == positions[None, :]
    ordered = jnp.sum(jnp.where(chosen, frame_counts[None, :], 0), axis=1)
    starts = (jnp.cumsum(ordered) - ordered) * NRB
    own_count = jnp.sum(jnp.where(positions == device, frame_counts, 0))

    active = normalize(latents.astype(jnp.float32), own_count, norm_scale, norm_offset).astype(
        jnp.bfloat16
    )
    padded = jnp.pad(active, ((2, 0), (1, 1), (1, 1), (0, 0)))
    unfolded = jnp.concatenate(
        [
            padded[:, row_tap : row_tap + frame_rows, col_tap : col_tap + columns]
            for row_tap in range(3)
            for col_tap in range(3)
        ],
        axis=-1,
    ).reshape(frames + 2, frame_rows * columns, 9 * channels)
    kernel = conv_weight.reshape(3, 9 * channels, -1)
    spread_out = [
        jnp.dot(
            unfolded.reshape(-1, 9 * channels), kernel[frame_lag], preferred_element_type=jnp.float32
        ).reshape(frames + 2, frame_rows * columns, -1)
        for frame_lag in range(3)
    ]
    conv = conv_bias + sum(
        spread_out[frame_lag][frame_lag : frame_lag + frames] for frame_lag in range(3)
    )
    conv = conv.reshape(frames, frame_rows, columns, -1)
    block_out = conv.astype(jnp.bfloat16)
    per_group = channels // GROUPS
    grouped = block_out.astype(jnp.float32).reshape(frames, frame_rows * columns, GROUPS, per_group)
    live_mask = (jnp.arange(frames) < own_count).astype(jnp.float32)[:, None, None, None]
    members = own_count.astype(jnp.float32) * (frame_rows * columns * per_group)
    first_sum = jnp.sum(grouped * live_mask, axis=(0, 1, 3))
    second_sum = jnp.sum(grouped * grouped * live_mask, axis=(0, 1, 3))
    clip_mean = first_sum / members
    clip_spread = second_sum / members - clip_mean * clip_mean
    clip_inverse = lax.rsqrt(clip_spread + eps)

    tiles = block_out.reshape(frames, NRB, tile_rows, columns, channels)
    tiles = jnp.pad(tiles, ((0, per_dest * classes - frames), (0, 0), (0, 0), (0, 0), (0, 0)))
    tiles = tiles.reshape(per_dest, classes, NRB, tile_rows, columns, channels)
    lag_of = (jnp.arange(classes, dtype=jnp.int32)[:, None] - (starts // NRB)[None, :] % classes) % classes
    pick = jnp.sum(jnp.where(clip_order[None, :] == device, lag_of, 0), axis=1)
    chosen = jnp.broadcast_to(tiles[:, 0:1], tiles.shape)
    for lag in range(1, classes):
        chosen = jnp.where(
            (pick == lag)[None, :, None, None, None, None], tiles[:, lag : lag + 1], chosen
        )
    tiles = chosen
    tiles = jnp.transpose(tiles, (1, 2, 3, 0, 4, 5)).reshape(
        devices, tile_rows * per_dest * columns, channels
    )
    stats = jnp.stack([clip_mean, clip_inverse], 0)
    stats = jnp.repeat(stats, per_group, axis=1)
    high = lax.reduce_precision(stats, exponent_bits=8, mantissa_bits=7)
    low = stats - high
    stat_rows = jnp.concatenate([high, low, jnp.zeros((4, channels), jnp.float32)], 0)
    stat_rows = jnp.broadcast_to(stat_rows.astype(jnp.bfloat16)[None], (devices, 8, channels))
    outgoing = jnp.concatenate([tiles, stat_rows], 1)
    received = lax.all_to_all(outgoing, "tile", split_axis=0, concat_axis=0, tiled=True)
    block_part = received[:, : per_dest * tile_rows * columns].reshape(
        devices, tile_rows, per_dest, columns, channels
    )
    stat_part = received[:, per_dest * tile_rows * columns :].astype(jnp.float32)
    src_mean = stat_part[:, 0] + stat_part[:, 2]
    src_inverse = stat_part[:, 1] + stat_part[:, 3]
    normed_part = (block_part.astype(jnp.float32) - src_mean[:, None, None, None, :]) * src_inverse[
        :, None, None, None, :
    ] * out_scale + out_offset
    normed_part = jax.nn.silu(normed_part).astype(jnp.bfloat16)

    local_slot = jnp.arange(worker_tiles, dtype=jnp.int32)
    tile_id = local_slot * devices + device
    placed = jnp.sum((starts[None, :] <= tile_id[:, None]).astype(jnp.int32), axis=1) - 1
    at_place = placed[:, None] == positions[None, :]
    clip_id = jnp.sum(jnp.where(at_place, clip_order[None, :], 0), axis=1)
    within = tile_id - jnp.sum(jnp.where(at_place, starts[None, :], 0), axis=1)
    row_of = jnp.arange(tile_rows, dtype=jnp.int32)[:, None]
    take_from = (clip_id[None, :] * tile_rows + row_of) * per_dest + (within // NRB // classes)[None, :]
    rows_all = devices * tile_rows * per_dest
    block_mine = jnp.take(block_part.reshape(rows_all, columns, channels), take_from, axis=0)
    normed_mine = jnp.take(normed_part.reshape(rows_all, columns, channels), take_from, axis=0)
    return (block_mine, normed_mine)


def solution(mesh):
    in_specs = (
        P(("grp", "tile"), None, None, None),
        P("grp"),
        P("grp"),
        P(),
        P(),
        P(),
        P(),
        P(),
        P(),
    )
    out_specs = (P(None, ("grp", "tile"), None, None), P(None, ("grp", "tile"), None, None))
    return jax.shard_map(local, mesh=mesh, in_specs=in_specs, out_specs=out_specs, check_vma=False)
```

```python
import jax
import jax.numpy as jnp
from jax import lax
from jax.sharding import PartitionSpec as P

GROUPS = 32
MEANF = 4
NRB = 8


eps = 1e-06


def normalize(values, live_frames, scaling, offsets):
    frames = values.shape[0]
    channels = values.shape[-1]
    flat = values.reshape(frames, -1, channels)
    live_mask = live_frames[:, None]
    members = jnp.sum(live_frames) * flat.shape[1] * (channels // GROUPS)
    first = jnp.sum(jnp.sum(flat, axis=1) * live_mask, axis=0)
    second = jnp.sum(jnp.sum(flat * flat, axis=1) * live_mask, axis=0)
    group_mean = jnp.sum(first.reshape(GROUPS, -1), axis=1) / members
    spread = jnp.sum(second.reshape(GROUPS, -1), axis=1) / members - group_mean * group_mean
    inverse = lax.rsqrt(spread + eps)
    grouped = values.reshape(frames, -1, GROUPS, channels // GROUPS)
    normed = (grouped - group_mean[:, None]) * inverse[:, None] * scaling.reshape(
        GROUPS, -1
    ) + offsets.reshape(GROUPS, -1)
    return jax.nn.silu(normed).reshape(values.shape)


def local(
    latents,
    frame_counts,
    clip_order,
    norm_scale,
    norm_offset,
    conv_weight,
    conv_bias,
    out_scale,
    out_offset,
):
    devices = lax.axis_size("tile")
    device = lax.axis_index("tile")
    frames, frame_rows, columns, channels = latents.shape
    tile_rows = frame_rows // NRB
    classes = devices // NRB
    per_dest = (frames + classes - 1) // classes
    worker_tiles = MEANF * NRB
    meta = lax.optimization_barrier(jnp.stack([frame_counts, clip_order], 0))
    frame_counts, clip_order = meta[0], meta[1]
    positions = jnp.arange(frame_counts.shape[0], dtype=jnp.int32)
    chosen = clip_order[:, None] == positions[None, :]
    ordered = jnp.sum(jnp.where(chosen, frame_counts[None, :], 0), axis=1)
    starts = (jnp.cumsum(ordered) - ordered) * NRB
    live_frames = jnp.sum(
        jnp.where(
            (positions[None, :] == device)
            & (jnp.arange(latents.shape[0], dtype=jnp.int32)[:, None] < frame_counts[None, :]),
            1.0,
            0.0,
        ),
        axis=1,
    )

    active = normalize(latents.astype(jnp.float32), live_frames, norm_scale, norm_offset).astype(
        jnp.bfloat16
    )
    padded = jnp.pad(active, ((2, 0), (1, 1), (1, 1), (0, 0)))
    unfolded = jnp.concatenate(
        [
            padded[:, row_tap : row_tap + frame_rows, col_tap : col_tap + columns]
            for row_tap in range(3)
            for col_tap in range(3)
        ],
        axis=-1,
    ).reshape(frames + 2, frame_rows * columns, 9 * channels)
    kernel = conv_weight.reshape(3, 9 * channels, -1)
    spread_out = [
        jnp.dot(
            unfolded.reshape(-1, 9 * channels), kernel[frame_lag], preferred_element_type=jnp.float32
        ).reshape(frames + 2, frame_rows * columns, -1)
        for frame_lag in range(3)
    ]
    conv = conv_bias + sum(
        spread_out[frame_lag][frame_lag : frame_lag + frames] for frame_lag in range(3)
    )
    conv = conv.reshape(frames, frame_rows, columns, -1)
    block_out = conv.astype(jnp.bfloat16)
    per_group = channels // GROUPS
    grouped = block_out.astype(jnp.float32).reshape(frames, frame_rows * columns, GROUPS, per_group)
    live_mask = live_frames[:, None, None, None]
    members = jnp.sum(live_frames) * (frame_rows * columns * per_group)
    first_sum = jnp.sum(grouped * live_mask, axis=(0, 1, 3))
    second_sum = jnp.sum(grouped * grouped * live_mask, axis=(0, 1, 3))
    clip_mean = first_sum / members
    clip_spread = second_sum / members - clip_mean * clip_mean
    clip_inverse = lax.rsqrt(clip_spread + eps)

    tiles = block_out.reshape(frames, NRB, tile_rows, columns, channels)
    tiles = jnp.pad(tiles, ((0, per_dest * classes - frames), (0, 0), (0, 0), (0, 0), (0, 0)))
    tiles = tiles.reshape(per_dest, classes, NRB, tile_rows, columns, channels)
    lag_of = (jnp.arange(classes, dtype=jnp.int32)[:, None] - (starts // NRB)[None, :] % classes) % classes
    pick = jnp.sum(jnp.where(clip_order[None, :] == device, lag_of, 0), axis=1)
    chosen = jnp.broadcast_to(tiles[:, 0:1], tiles.shape)
    for lag in range(1, classes):
        chosen = jnp.where(
            (pick == lag)[None, :, None, None, None, None], tiles[:, lag : lag + 1], chosen
        )
    tiles = chosen
    tiles = jnp.transpose(tiles, (1, 2, 3, 0, 4, 5)).reshape(
        devices, tile_rows * per_dest * columns, channels
    )
    stats = jnp.stack([clip_mean, clip_inverse], 0)
    stats = jnp.repeat(stats, per_group, axis=1)
    high = lax.reduce_precision(stats, exponent_bits=8, mantissa_bits=7)
    low = stats - high
    stat_rows = jnp.concatenate([high, low, jnp.zeros((4, channels), jnp.float32)], 0)
    stat_rows = jnp.broadcast_to(stat_rows.astype(jnp.bfloat16)[None], (devices, 8, channels))
    outgoing = jnp.concatenate([tiles, stat_rows], 1)
    received = lax.all_to_all(outgoing, "tile", split_axis=0, concat_axis=0, tiled=True)
    block_part = received[:, : per_dest * tile_rows * columns].reshape(
        devices, tile_rows, per_dest, columns, channels
    )
    stat_part = received[:, per_dest * tile_rows * columns :].astype(jnp.float32)
    src_mean = stat_part[:, 0] + stat_part[:, 2]
    src_inverse = stat_part[:, 1] + stat_part[:, 3]
    normed_part = (block_part.astype(jnp.float32) - src_mean[:, None, None, None, :]) * src_inverse[
        :, None, None, None, :
    ] * out_scale + out_offset
    normed_part = jax.nn.silu(normed_part).astype(jnp.bfloat16)

    local_slot = jnp.arange(worker_tiles, dtype=jnp.int32)
    tile_id = local_slot * devices + device
    placed = jnp.sum((starts[None, :] <= tile_id[:, None]).astype(jnp.int32), axis=1) - 1
    at_place = placed[:, None] == positions[None, :]
    clip_id = jnp.sum(jnp.where(at_place, clip_order[None, :], 0), axis=1)
    within = tile_id - jnp.sum(jnp.where(at_place, starts[None, :], 0), axis=1)
    row_of = jnp.arange(tile_rows, dtype=jnp.int32)[:, None]
    take_from = (clip_id[None, :] * tile_rows + row_of) * per_dest + (within // NRB // classes)[None, :]
    rows_all = devices * tile_rows * per_dest
    block_mine = jnp.take(block_part.reshape(rows_all, columns, channels), take_from, axis=0)
    normed_mine = jnp.take(normed_part.reshape(rows_all, columns, channels), take_from, axis=0)
    return (block_mine, normed_mine)


def solution(mesh):
    in_specs = (
        P(("grp", "tile"), None, None, None),
        P("grp"),
        P("grp"),
        P(),
        P(),
        P(),
        P(),
        P(),
        P(),
    )
    out_specs = (P(None, ("grp", "tile"), None, None), P(None, ("grp", "tile"), None, None))
    return jax.shard_map(local, mesh=mesh, in_specs=in_specs, out_specs=out_specs, check_vma=False)
```

```python
import jax
import jax.numpy as jnp
from jax import lax
from jax.sharding import PartitionSpec as P

GROUPS = 32
MEANF = 4
NRB = 8


eps = 1e-06


def normalize(values, live_frames, scaling, offsets):
    frames = values.shape[0]
    channels = values.shape[-1]
    flat = values.reshape(frames, -1, channels)
    live_mask = live_frames[:, None]
    members = jnp.sum(live_frames) * flat.shape[1] * (channels // GROUPS)
    first = jnp.sum(jnp.sum(flat, axis=1) * live_mask, axis=0)
    second = jnp.sum(jnp.sum(flat * flat, axis=1) * live_mask, axis=0)
    group_mean = jnp.sum(first.reshape(GROUPS, -1), axis=1) / members
    spread = jnp.sum(second.reshape(GROUPS, -1), axis=1) / members - group_mean * group_mean
    inverse = lax.rsqrt(spread + eps)
    grouped = values.reshape(frames, -1, GROUPS, channels // GROUPS)
    normed = (grouped - group_mean[:, None]) * inverse[:, None] * scaling.reshape(
        GROUPS, -1
    ) + offsets.reshape(GROUPS, -1)
    return jax.nn.silu(normed).reshape(values.shape)


def local(
    latents,
    frame_counts,
    clip_order,
    norm_scale,
    norm_offset,
    conv_weight,
    conv_bias,
    out_scale,
    out_offset,
):
    devices = lax.axis_size("tile")
    device = lax.axis_index("tile")
    frames, frame_rows, columns, channels = latents.shape
    tile_rows = frame_rows // NRB
    classes = devices // NRB
    per_dest = (frames + classes - 1) // classes
    worker_tiles = MEANF * NRB
    meta = lax.optimization_barrier(jnp.stack([frame_counts, clip_order], 0))
    frame_counts, clip_order = meta[0], meta[1]
    positions = jnp.arange(frame_counts.shape[0], dtype=jnp.int32)
    chosen = clip_order[:, None] == positions[None, :]
    ordered = jnp.sum(jnp.where(chosen, frame_counts[None, :], 0), axis=1)
    starts = (jnp.cumsum(ordered) - ordered) * NRB
    live_frames = jnp.sum(
        jnp.where(
            (positions[None, :] == device)
            & (jnp.arange(latents.shape[0], dtype=jnp.int32)[:, None] < frame_counts[None, :]),
            1.0,
            0.0,
        ),
        axis=1,
    )

    active = normalize(latents.astype(jnp.float32), live_frames, norm_scale, norm_offset).astype(
        jnp.bfloat16
    )
    padded = jnp.pad(active, ((2, 0), (1, 1), (1, 1), (0, 0)))
    unfolded = jnp.concatenate(
        [
            padded[:, row_tap : row_tap + frame_rows, col_tap : col_tap + columns]
            for row_tap in range(3)
            for col_tap in range(3)
        ],
        axis=-1,
    ).reshape(frames + 2, frame_rows * columns, 9 * channels)
    kernel = conv_weight.reshape(3, 9 * channels, -1)
    spread_out = [
        jnp.dot(
            unfolded.reshape(-1, 9 * channels), kernel[frame_lag], preferred_element_type=jnp.float32
        ).reshape(frames + 2, frame_rows * columns, -1)
        for frame_lag in range(3)
    ]
    conv = conv_bias + sum(
        spread_out[frame_lag][frame_lag : frame_lag + frames] for frame_lag in range(3)
    )
    conv = conv.reshape(frames, frame_rows, columns, -1)
    block_out = conv.astype(jnp.bfloat16)
    per_group = channels // GROUPS
    grouped = block_out.astype(jnp.float32).reshape(frames, frame_rows * columns, GROUPS, per_group)
    live_mask = live_frames[:, None, None, None]
    members = jnp.sum(live_frames) * (frame_rows * columns * per_group)
    first_sum = jnp.sum(grouped * live_mask, axis=(0, 1, 3))
    second_sum = jnp.sum(grouped * grouped * live_mask, axis=(0, 1, 3))
    clip_mean = first_sum / members
    clip_spread = second_sum / members - clip_mean * clip_mean
    clip_inverse = lax.rsqrt(clip_spread + eps)

    tiles = block_out.reshape(frames, NRB, tile_rows, columns, channels)
    tiles = jnp.pad(tiles, ((0, per_dest * classes - frames), (0, 0), (0, 0), (0, 0), (0, 0)))
    tiles = tiles.reshape(per_dest, classes, NRB, tile_rows, columns, channels)
    lag_of = (jnp.arange(classes, dtype=jnp.int32)[:, None] - (starts // NRB)[None, :] % classes) % classes
    pick = jnp.sum(jnp.where(clip_order[None, :] == device, lag_of, 0), axis=1)
    chosen = jnp.broadcast_to(tiles[:, 0:1], tiles.shape)
    for lag in range(1, classes):
        chosen = jnp.where(
            (pick == lag)[None, :, None, None, None, None], tiles[:, lag : lag + 1], chosen
        )
    tiles = chosen
    tiles = jnp.transpose(tiles, (1, 2, 3, 0, 4, 5)).reshape(
        devices, tile_rows * per_dest * columns, channels
    )
    stats = jnp.stack([clip_mean, clip_inverse], 0)
    stats = jnp.repeat(stats, per_group, axis=1)
    high = lax.reduce_precision(stats, exponent_bits=8, mantissa_bits=7)
    low = stats - high
    stat_rows = jnp.concatenate([high, low, jnp.zeros((4, channels), jnp.float32)], 0)
    stat_rows = jnp.broadcast_to(stat_rows.astype(jnp.bfloat16)[None], (devices, 8, channels))
    outgoing = jnp.concatenate([tiles, stat_rows], 1)
    received = lax.all_to_all(outgoing, "tile", split_axis=0, concat_axis=0, tiled=True)
    block_part = received[:, : per_dest * tile_rows * columns].reshape(
        devices, tile_rows, per_dest, columns, channels
    )
    stat_part = received[:, per_dest * tile_rows * columns :].astype(jnp.float32)
    src_mean = stat_part[:, 0] + stat_part[:, 2]
    src_inverse = stat_part[:, 1] + stat_part[:, 3]
    normed_part = (block_part.astype(jnp.float32) - src_mean[:, None, None, None, :]) * src_inverse[
        :, None, None, None, :
    ] * out_scale + out_offset
    normed_part = jax.nn.silu(normed_part).astype(jnp.bfloat16)

    local_slot = jnp.arange(worker_tiles, dtype=jnp.int32)
    tile_id = local_slot * devices + device
    placed = jnp.sum((starts[None, :] <= tile_id[:, None]).astype(jnp.int32), axis=1) - 1
    at_place = placed[:, None] == positions[None, :]
    clip_id = jnp.sum(jnp.where(at_place, clip_order[None, :], 0), axis=1)
    within = tile_id - jnp.sum(jnp.where(at_place, starts[None, :], 0), axis=1)
    row_of = jnp.arange(tile_rows, dtype=jnp.int32)[:, None]
    take_from = (clip_id[None, :] * tile_rows + row_of) * per_dest + (within // NRB // classes)[None, :]
    rows_all = devices * tile_rows * per_dest
    both = jnp.stack([block_part, normed_part], 0).reshape(2 * rows_all, columns, channels)
    picked = jnp.take(both, jnp.stack([take_from, take_from + rows_all], 0), axis=0, mode="clip")
    return (picked[0], picked[1])


def solution(mesh):
    in_specs = (
        P(("grp", "tile"), None, None, None),
        P("grp"),
        P("grp"),
        P(),
        P(),
        P(),
        P(),
        P(),
        P(),
    )
    out_specs = (P(None, ("grp", "tile"), None, None), P(None, ("grp", "tile"), None, None))
    return jax.shard_map(local, mesh=mesh, in_specs=in_specs, out_specs=out_specs, check_vma=False)
```

```python
import jax
import jax.numpy as jnp
from jax import lax
from jax.sharding import PartitionSpec as P

GROUPS = 32
MEANF = 4
NRB = 8


eps = 1e-06


def normalize(values, live_frames, scaling, offsets):
    frames = values.shape[0]
    channels = values.shape[-1]
    flat = values.reshape(frames, -1, channels)
    live_mask = live_frames[:, None]
    members = jnp.sum(live_frames) * flat.shape[1] * (channels // GROUPS)
    first = jnp.sum(jnp.sum(flat, axis=1) * live_mask, axis=0)
    second = jnp.sum(jnp.sum(flat * flat, axis=1) * live_mask, axis=0)
    group_mean = jnp.sum(first.reshape(GROUPS, -1), axis=1) / members
    spread = jnp.sum(second.reshape(GROUPS, -1), axis=1) / members - group_mean * group_mean
    inverse = lax.rsqrt(spread + eps)
    grouped = values.reshape(frames, -1, GROUPS, channels // GROUPS)
    normed = (grouped - group_mean[:, None]) * inverse[:, None] * scaling.reshape(
        GROUPS, -1
    ) + offsets.reshape(GROUPS, -1)
    return jax.nn.silu(normed).reshape(values.shape)


def local(
    latents,
    frame_counts,
    clip_order,
    norm_scale,
    norm_offset,
    conv_weight,
    conv_bias,
    out_scale,
    out_offset,
):
    devices = lax.axis_size("tile")
    device = lax.axis_index("tile")
    frames, frame_rows, columns, channels = latents.shape
    tile_rows = frame_rows // NRB
    classes = devices // NRB
    per_dest = (frames + classes - 1) // classes
    worker_tiles = MEANF * NRB
    meta = lax.optimization_barrier(jnp.stack([frame_counts, clip_order], 0))
    frame_counts, clip_order = meta[0], meta[1]
    positions = jnp.arange(frame_counts.shape[0], dtype=jnp.int32)
    chosen = clip_order[:, None] == positions[None, :]
    ordered = jnp.sum(jnp.where(chosen, frame_counts[None, :], 0), axis=1)
    starts = (jnp.cumsum(ordered) - ordered) * NRB
    live_frames = jnp.sum(
        jnp.where(
            (positions[None, :] == device)
            & (jnp.arange(latents.shape[0], dtype=jnp.int32)[:, None] < frame_counts[None, :]),
            1.0,
            0.0,
        ),
        axis=1,
    )

    active = normalize(latents.astype(jnp.float32), live_frames, norm_scale, norm_offset).astype(
        jnp.bfloat16
    )
    padded = jnp.pad(active, ((2, 0), (1, 1), (1, 1), (0, 0)))
    unfolded = jnp.concatenate(
        [
            padded[:, row_tap : row_tap + frame_rows, col_tap : col_tap + columns]
            for row_tap in range(3)
            for col_tap in range(3)
        ],
        axis=-1,
    ).reshape(frames + 2, frame_rows * columns, 9 * channels)
    kernel = conv_weight.reshape(3, 9 * channels, -1)
    spread_out = lax.dot_general(
        unfolded.reshape(-1, 9 * channels),
        kernel,
        (((1,), (1,)), ((), ())),
        preferred_element_type=jnp.float32,
    ).reshape(frames + 2, frame_rows * columns, 3, -1)
    conv = conv_bias + sum(
        spread_out[frame_lag : frame_lag + frames, :, frame_lag] for frame_lag in range(3)
    )
    conv = conv.reshape(frames, frame_rows, columns, -1)
    block_out = conv.astype(jnp.bfloat16)
    per_group = channels // GROUPS
    grouped = block_out.astype(jnp.float32).reshape(frames, frame_rows * columns, GROUPS, per_group)
    live_mask = live_frames[:, None, None, None]
    members = jnp.sum(live_frames) * (frame_rows * columns * per_group)
    first_sum = jnp.sum(grouped * live_mask, axis=(0, 1, 3))
    second_sum = jnp.sum(grouped * grouped * live_mask, axis=(0, 1, 3))
    clip_mean = first_sum / members
    clip_spread = second_sum / members - clip_mean * clip_mean
    clip_inverse = lax.rsqrt(clip_spread + eps)

    tiles = block_out.reshape(frames, NRB, tile_rows, columns, channels)
    tiles = jnp.pad(tiles, ((0, per_dest * classes - frames), (0, 0), (0, 0), (0, 0), (0, 0)))
    tiles = tiles.reshape(per_dest, classes, NRB, tile_rows, columns, channels)
    lag_of = (jnp.arange(classes, dtype=jnp.int32)[:, None] - (starts // NRB)[None, :] % classes) % classes
    pick = jnp.sum(jnp.where(clip_order[None, :] == device, lag_of, 0), axis=1)
    chosen = jnp.broadcast_to(tiles[:, 0:1], tiles.shape)
    for lag in range(1, classes):
        chosen = jnp.where(
            (pick == lag)[None, :, None, None, None, None], tiles[:, lag : lag + 1], chosen
        )
    tiles = chosen
    tiles = jnp.transpose(tiles, (1, 2, 3, 0, 4, 5)).reshape(
        devices, tile_rows * per_dest * columns, channels
    )
    stats = jnp.stack([clip_mean, clip_inverse], 0)
    stats = jnp.repeat(stats, per_group, axis=1)
    high = lax.reduce_precision(stats, exponent_bits=8, mantissa_bits=7)
    low = stats - high
    stat_rows = jnp.concatenate([high, low, jnp.zeros((4, channels), jnp.float32)], 0)
    stat_rows = jnp.broadcast_to(stat_rows.astype(jnp.bfloat16)[None], (devices, 8, channels))
    outgoing = jnp.concatenate([tiles, stat_rows], 1)
    received = lax.all_to_all(outgoing, "tile", split_axis=0, concat_axis=0, tiled=True)
    block_part = received[:, : per_dest * tile_rows * columns].reshape(
        devices, tile_rows, per_dest, columns, channels
    )
    stat_part = received[:, per_dest * tile_rows * columns :].astype(jnp.float32)
    src_mean = stat_part[:, 0] + stat_part[:, 2]
    src_inverse = stat_part[:, 1] + stat_part[:, 3]
    normed_part = (block_part.astype(jnp.float32) - src_mean[:, None, None, None, :]) * src_inverse[
        :, None, None, None, :
    ] * out_scale + out_offset
    normed_part = jax.nn.silu(normed_part).astype(jnp.bfloat16)

    local_slot = jnp.arange(worker_tiles, dtype=jnp.int32)
    tile_id = local_slot * devices + device
    placed = jnp.sum((starts[None, :] <= tile_id[:, None]).astype(jnp.int32), axis=1) - 1
    at_place = placed[:, None] == positions[None, :]
    clip_id = jnp.sum(jnp.where(at_place, clip_order[None, :], 0), axis=1)
    within = tile_id - jnp.sum(jnp.where(at_place, starts[None, :], 0), axis=1)
    row_of = jnp.arange(tile_rows, dtype=jnp.int32)[:, None]
    take_from = (clip_id[None, :] * tile_rows + row_of) * per_dest + (within // NRB // classes)[None, :]
    rows_all = devices * tile_rows * per_dest
    both = jnp.stack([block_part, normed_part], 0).reshape(2 * rows_all, columns, channels)
    picked = jnp.take(both, jnp.stack([take_from, take_from + rows_all], 0), axis=0, mode="clip")
    return (picked[0], picked[1])


def solution(mesh):
    in_specs = (
        P(("grp", "tile"), None, None, None),
        P("grp"),
        P("grp"),
        P(),
        P(),
        P(),
        P(),
        P(),
        P(),
    )
    out_specs = (P(None, ("grp", "tile"), None, None), P(None, ("grp", "tile"), None, None))
    return jax.shard_map(local, mesh=mesh, in_specs=in_specs, out_specs=out_specs, check_vma=False)
```

```python
import jax
import jax.numpy as jnp
from jax import lax
from jax.sharding import PartitionSpec as P

GROUPS = 32
MEANF = 4
NRB = 8


eps = 1e-06


def normalize(values, live_frames, scaling, offsets):
    frames = values.shape[0]
    channels = values.shape[-1]
    flat = values.reshape(frames, -1, channels)
    live_mask = live_frames[:, None]
    members = jnp.sum(live_frames) * flat.shape[1] * (channels // GROUPS)
    first = jnp.sum(jnp.sum(flat, axis=1) * live_mask, axis=0)
    second = jnp.sum(jnp.sum(flat * flat, axis=1) * live_mask, axis=0)
    group_mean = jnp.sum(first.reshape(GROUPS, -1), axis=1) / members
    spread = jnp.sum(second.reshape(GROUPS, -1), axis=1) / members - group_mean * group_mean
    inverse = lax.rsqrt(spread + eps)
    grouped = values.reshape(frames, -1, GROUPS, channels // GROUPS)
    normed = (grouped - group_mean[:, None]) * inverse[:, None] * scaling.reshape(
        GROUPS, -1
    ) + offsets.reshape(GROUPS, -1)
    return jax.nn.silu(normed).reshape(values.shape)


def local(
    latents,
    frame_counts,
    clip_order,
    norm_scale,
    norm_offset,
    conv_weight,
    conv_bias,
    out_scale,
    out_offset,
):
    devices = lax.axis_size("tile")
    device = lax.axis_index("tile")
    frames, frame_rows, columns, channels = latents.shape
    tile_rows = frame_rows // NRB
    classes = devices // NRB
    per_dest = (frames + classes - 1) // classes
    worker_tiles = MEANF * NRB
    meta = lax.optimization_barrier(jnp.stack([frame_counts, clip_order], 0))
    frame_counts, clip_order = meta[0], meta[1]
    positions = jnp.arange(frame_counts.shape[0], dtype=jnp.int32)
    chosen = clip_order[:, None] == positions[None, :]
    ordered = jnp.sum(jnp.where(chosen, frame_counts[None, :], 0), axis=1)
    starts = (jnp.cumsum(ordered) - ordered) * NRB
    live_frames = jnp.sum(
        jnp.where(
            (positions[None, :] == device)
            & (jnp.arange(latents.shape[0], dtype=jnp.int32)[:, None] < frame_counts[None, :]),
            1.0,
            0.0,
        ),
        axis=1,
    )

    active = normalize(latents.astype(jnp.float32), live_frames, norm_scale, norm_offset).astype(
        jnp.bfloat16
    )
    padded = jnp.pad(active, ((2, 0), (1, 1), (1, 1), (0, 0)))
    unfolded = jnp.concatenate(
        [
            padded[:, row_tap : row_tap + frame_rows, col_tap : col_tap + columns]
            for row_tap in range(3)
            for col_tap in range(3)
        ],
        axis=-1,
    ).reshape(frames + 2, frame_rows * columns, 9 * channels)
    kernel = conv_weight.reshape(3, 9 * channels, -1)
    flat_in = unfolded.reshape(-1, 9 * channels)
    spread_out = lax.dot_general(
        jnp.broadcast_to(flat_in[None], (3,) + flat_in.shape),
        kernel,
        (((2,), (1,)), ((0,), (0,))),
        preferred_element_type=jnp.float32,
    ).reshape(3, frames + 2, frame_rows * columns, -1)
    conv = conv_bias + sum(
        spread_out[frame_lag, frame_lag : frame_lag + frames] for frame_lag in range(3)
    )
    conv = conv.reshape(frames, frame_rows, columns, -1)
    block_out = conv.astype(jnp.bfloat16)
    per_group = channels // GROUPS
    grouped = block_out.astype(jnp.float32).reshape(frames, frame_rows * columns, GROUPS, per_group)
    live_mask = live_frames[:, None, None, None]
    members = jnp.sum(live_frames) * (frame_rows * columns * per_group)
    first_sum = jnp.sum(grouped * live_mask, axis=(0, 1, 3))
    second_sum = jnp.sum(grouped * grouped * live_mask, axis=(0, 1, 3))
    clip_mean = first_sum / members
    clip_spread = second_sum / members - clip_mean * clip_mean
    clip_inverse = lax.rsqrt(clip_spread + eps)

    tiles = block_out.reshape(frames, NRB, tile_rows, columns, channels)
    tiles = jnp.pad(tiles, ((0, per_dest * classes - frames), (0, 0), (0, 0), (0, 0), (0, 0)))
    tiles = tiles.reshape(per_dest, classes, NRB, tile_rows, columns, channels)
    lag_of = (jnp.arange(classes, dtype=jnp.int32)[:, None] - (starts // NRB)[None, :] % classes) % classes
    pick = jnp.sum(jnp.where(clip_order[None, :] == device, lag_of, 0), axis=1)
    chosen = jnp.broadcast_to(tiles[:, 0:1], tiles.shape)
    for lag in range(1, classes):
        chosen = jnp.where(
            (pick == lag)[None, :, None, None, None, None], tiles[:, lag : lag + 1], chosen
        )
    tiles = chosen
    tiles = jnp.transpose(tiles, (1, 2, 3, 0, 4, 5)).reshape(
        devices, tile_rows * per_dest * columns, channels
    )
    stats = jnp.stack([clip_mean, clip_inverse], 0)
    stats = jnp.repeat(stats, per_group, axis=1)
    high = lax.reduce_precision(stats, exponent_bits=8, mantissa_bits=7)
    low = stats - high
    stat_rows = jnp.concatenate([high, low, jnp.zeros((4, channels), jnp.float32)], 0)
    stat_rows = jnp.broadcast_to(stat_rows.astype(jnp.bfloat16)[None], (devices, 8, channels))
    outgoing = jnp.concatenate([tiles, stat_rows], 1)
    received = lax.all_to_all(outgoing, "tile", split_axis=0, concat_axis=0, tiled=True)
    block_part = received[:, : per_dest * tile_rows * columns].reshape(
        devices, tile_rows, per_dest, columns, channels
    )
    stat_part = received[:, per_dest * tile_rows * columns :].astype(jnp.float32)
    src_mean = stat_part[:, 0] + stat_part[:, 2]
    src_inverse = stat_part[:, 1] + stat_part[:, 3]
    normed_part = (block_part.astype(jnp.float32) - src_mean[:, None, None, None, :]) * src_inverse[
        :, None, None, None, :
    ] * out_scale + out_offset
    normed_part = jax.nn.silu(normed_part).astype(jnp.bfloat16)

    local_slot = jnp.arange(worker_tiles, dtype=jnp.int32)
    tile_id = local_slot * devices + device
    placed = jnp.sum((starts[None, :] <= tile_id[:, None]).astype(jnp.int32), axis=1) - 1
    at_place = placed[:, None] == positions[None, :]
    clip_id = jnp.sum(jnp.where(at_place, clip_order[None, :], 0), axis=1)
    within = tile_id - jnp.sum(jnp.where(at_place, starts[None, :], 0), axis=1)
    row_of = jnp.arange(tile_rows, dtype=jnp.int32)[:, None]
    take_from = (clip_id[None, :] * tile_rows + row_of) * per_dest + (within // NRB // classes)[None, :]
    rows_all = devices * tile_rows * per_dest
    both = jnp.stack([block_part, normed_part], 0).reshape(2 * rows_all, columns, channels)
    picked = jnp.take(both, jnp.stack([take_from, take_from + rows_all], 0), axis=0, mode="clip")
    return (picked[0], picked[1])


def solution(mesh):
    in_specs = (
        P(("grp", "tile"), None, None, None),
        P("grp"),
        P("grp"),
        P(),
        P(),
        P(),
        P(),
        P(),
        P(),
    )
    out_specs = (P(None, ("grp", "tile"), None, None), P(None, ("grp", "tile"), None, None))
    return jax.shard_map(local, mesh=mesh, in_specs=in_specs, out_specs=out_specs, check_vma=False)
```

```python
import jax
import jax.numpy as jnp
from jax import lax
from jax.sharding import PartitionSpec as P

GROUPS = 32
MEANF = 4
NRB = 8


eps = 1e-06


def normalize(values, live_frames, scaling, offsets):
    frames = values.shape[0]
    channels = values.shape[-1]
    flat = values.reshape(frames, -1, channels)
    live_mask = live_frames[:, None]
    members = jnp.sum(live_frames) * flat.shape[1] * (channels // GROUPS)
    first = jnp.sum(jnp.sum(flat, axis=1) * live_mask, axis=0)
    second = jnp.sum(jnp.sum(flat * flat, axis=1) * live_mask, axis=0)
    group_mean = jnp.sum(first.reshape(GROUPS, -1), axis=1) / members
    spread = jnp.sum(second.reshape(GROUPS, -1), axis=1) / members - group_mean * group_mean
    inverse = lax.rsqrt(spread + eps)
    grouped = values.reshape(frames, -1, GROUPS, channels // GROUPS)
    normed = (grouped - group_mean[:, None]) * inverse[:, None] * scaling.reshape(
        GROUPS, -1
    ) + offsets.reshape(GROUPS, -1)
    return jax.nn.silu(normed).reshape(values.shape)


def local(
    latents,
    frame_counts,
    clip_order,
    norm_scale,
    norm_offset,
    conv_weight,
    conv_bias,
    out_scale,
    out_offset,
):
    devices = lax.axis_size("tile")
    device = lax.axis_index("tile")
    frames, frame_rows, columns, channels = latents.shape
    tile_rows = frame_rows // NRB
    classes = devices // NRB
    per_dest = (frames + classes - 1) // classes
    worker_tiles = MEANF * NRB
    meta = lax.optimization_barrier(jnp.stack([frame_counts, clip_order], 0))
    frame_counts, clip_order = meta[0], meta[1]
    positions = jnp.arange(frame_counts.shape[0], dtype=jnp.int32)
    chosen = clip_order[:, None] == positions[None, :]
    ordered = jnp.sum(jnp.where(chosen, frame_counts[None, :], 0), axis=1)
    starts = (jnp.cumsum(ordered) - ordered) * NRB
    live_frames = jnp.sum(
        jnp.where(
            (positions[None, :] == device)
            & (jnp.arange(latents.shape[0], dtype=jnp.int32)[:, None] < frame_counts[None, :]),
            1.0,
            0.0,
        ),
        axis=1,
    )

    active = normalize(latents.astype(jnp.float32), live_frames, norm_scale, norm_offset).astype(
        jnp.bfloat16
    )
    padded = jnp.pad(active, ((0, 0), (1, 1), (1, 1), (0, 0)))
    unfolded = jnp.concatenate(
        [
            padded[:, row_tap : row_tap + frame_rows, col_tap : col_tap + columns]
            for row_tap in range(3)
            for col_tap in range(3)
        ],
        axis=-1,
    ).reshape(frames * frame_rows * columns, 9 * channels)
    kernel = conv_weight.reshape(3, 9 * channels, -1)
    spread_out = [
        jnp.pad(
            jnp.dot(unfolded, kernel[frame_lag], preferred_element_type=jnp.float32).reshape(
                frames, frame_rows * columns, -1
            ),
            ((2 - frame_lag, 0), (0, 0), (0, 0)),
        )[:frames]
        for frame_lag in range(3)
    ]
    conv = conv_bias + sum(spread_out)
    conv = conv.reshape(frames, frame_rows, columns, -1)
    block_out = conv.astype(jnp.bfloat16)
    per_group = channels // GROUPS
    grouped = block_out.astype(jnp.float32).reshape(frames, frame_rows * columns, GROUPS, per_group)
    live_mask = live_frames[:, None, None, None]
    members = jnp.sum(live_frames) * (frame_rows * columns * per_group)
    first_sum = jnp.sum(grouped * live_mask, axis=(0, 1, 3))
    second_sum = jnp.sum(grouped * grouped * live_mask, axis=(0, 1, 3))
    clip_mean = first_sum / members
    clip_spread = second_sum / members - clip_mean * clip_mean
    clip_inverse = lax.rsqrt(clip_spread + eps)

    tiles = block_out.reshape(frames, NRB, tile_rows, columns, channels)
    tiles = jnp.pad(tiles, ((0, per_dest * classes - frames), (0, 0), (0, 0), (0, 0), (0, 0)))
    tiles = tiles.reshape(per_dest, classes, NRB, tile_rows, columns, channels)
    lag_of = (jnp.arange(classes, dtype=jnp.int32)[:, None] - (starts // NRB)[None, :] % classes) % classes
    pick = jnp.sum(jnp.where(clip_order[None, :] == device, lag_of, 0), axis=1)
    chosen = jnp.broadcast_to(tiles[:, 0:1], tiles.shape)
    for lag in range(1, classes):
        chosen = jnp.where(
            (pick == lag)[None, :, None, None, None, None], tiles[:, lag : lag + 1], chosen
        )
    tiles = chosen
    tiles = jnp.transpose(tiles, (1, 2, 3, 0, 4, 5)).reshape(
        devices, tile_rows * per_dest * columns, channels
    )
    stats = jnp.stack([clip_mean, clip_inverse], 0)
    stats = jnp.repeat(stats, per_group, axis=1)
    high = lax.reduce_precision(stats, exponent_bits=8, mantissa_bits=7)
    low = stats - high
    stat_rows = jnp.concatenate([high, low, jnp.zeros((4, channels), jnp.float32)], 0)
    stat_rows = jnp.broadcast_to(stat_rows.astype(jnp.bfloat16)[None], (devices, 8, channels))
    outgoing = jnp.concatenate([tiles, stat_rows], 1)
    received = lax.all_to_all(outgoing, "tile", split_axis=0, concat_axis=0, tiled=True)
    block_part = received[:, : per_dest * tile_rows * columns].reshape(
        devices, tile_rows, per_dest, columns, channels
    )
    stat_part = received[:, per_dest * tile_rows * columns :].astype(jnp.float32)
    src_mean = stat_part[:, 0] + stat_part[:, 2]
    src_inverse = stat_part[:, 1] + stat_part[:, 3]
    normed_part = (block_part.astype(jnp.float32) - src_mean[:, None, None, None, :]) * src_inverse[
        :, None, None, None, :
    ] * out_scale + out_offset
    normed_part = jax.nn.silu(normed_part).astype(jnp.bfloat16)

    local_slot = jnp.arange(worker_tiles, dtype=jnp.int32)
    tile_id = local_slot * devices + device
    placed = jnp.sum((starts[None, :] <= tile_id[:, None]).astype(jnp.int32), axis=1) - 1
    at_place = placed[:, None] == positions[None, :]
    clip_id = jnp.sum(jnp.where(at_place, clip_order[None, :], 0), axis=1)
    within = tile_id - jnp.sum(jnp.where(at_place, starts[None, :], 0), axis=1)
    row_of = jnp.arange(tile_rows, dtype=jnp.int32)[:, None]
    take_from = (clip_id[None, :] * tile_rows + row_of) * per_dest + (within // NRB // classes)[None, :]
    rows_all = devices * tile_rows * per_dest
    both = jnp.stack([block_part, normed_part], 0).reshape(2 * rows_all, columns, channels)
    picked = jnp.take(both, jnp.stack([take_from, take_from + rows_all], 0), axis=0, mode="clip")
    return (picked[0], picked[1])


def solution(mesh):
    in_specs = (
        P(("grp", "tile"), None, None, None),
        P("grp"),
        P("grp"),
        P(),
        P(),
        P(),
        P(),
        P(),
        P(),
    )
    out_specs = (P(None, ("grp", "tile"), None, None), P(None, ("grp", "tile"), None, None))
    return jax.shard_map(local, mesh=mesh, in_specs=in_specs, out_specs=out_specs, check_vma=False)
```

```python
import jax
import jax.numpy as jnp
from jax import lax
from jax.sharding import PartitionSpec as P

GROUPS = 32
MEANF = 4
NRB = 8


eps = 1e-06


def normalize(values, live_frames, scaling, offsets):
    frames = values.shape[0]
    channels = values.shape[-1]
    flat = values.reshape(frames, -1, channels)
    live_mask = live_frames[:, None]
    members = jnp.sum(live_frames) * flat.shape[1] * (channels // GROUPS)
    first = jnp.sum(jnp.sum(flat, axis=1) * live_mask, axis=0)
    second = jnp.sum(jnp.sum(flat * flat, axis=1) * live_mask, axis=0)
    group_mean = jnp.sum(first.reshape(GROUPS, -1), axis=1) / members
    spread = jnp.sum(second.reshape(GROUPS, -1), axis=1) / members - group_mean * group_mean
    inverse = lax.rsqrt(spread + eps)
    grouped = values.reshape(frames, -1, GROUPS, channels // GROUPS)
    normed = (grouped - group_mean[:, None]) * inverse[:, None] * scaling.reshape(
        GROUPS, -1
    ) + offsets.reshape(GROUPS, -1)
    return jax.nn.silu(normed).reshape(values.shape)


def local(
    latents,
    frame_counts,
    clip_order,
    norm_scale,
    norm_offset,
    conv_weight,
    conv_bias,
    out_scale,
    out_offset,
):
    devices = lax.axis_size("tile")
    device = lax.axis_index("tile")
    frames, frame_rows, columns, channels = latents.shape
    tile_rows = frame_rows // NRB
    classes = devices // NRB
    per_dest = (frames + classes - 1) // classes
    worker_tiles = MEANF * NRB
    meta = lax.optimization_barrier(jnp.stack([frame_counts, clip_order], 0))
    frame_counts, clip_order = meta[0], meta[1]
    positions = jnp.arange(frame_counts.shape[0], dtype=jnp.int32)
    chosen = clip_order[:, None] == positions[None, :]
    ordered = jnp.sum(jnp.where(chosen, frame_counts[None, :], 0), axis=1)
    starts = (jnp.cumsum(ordered) - ordered) * NRB
    live_frames = jnp.sum(
        jnp.where(
            (positions[None, :] == device)
            & (jnp.arange(latents.shape[0], dtype=jnp.int32)[:, None] < frame_counts[None, :]),
            1.0,
            0.0,
        ),
        axis=1,
    )

    active = normalize(latents.astype(jnp.float32), live_frames, norm_scale, norm_offset).astype(
        jnp.bfloat16
    )
    padded = jnp.pad(active, ((2, 0), (1, 1), (1, 1), (0, 0)))
    unfolded = jnp.concatenate(
        [
            padded[:, row_tap : row_tap + frame_rows, col_tap : col_tap + columns]
            for row_tap in range(3)
            for col_tap in range(3)
        ],
        axis=-1,
    ).reshape(frames + 2, frame_rows * columns, 9 * channels)
    kernel = conv_weight.reshape(3, 9 * channels, -1)
    spread_out = [
        jnp.dot(
            unfolded.reshape(-1, 9 * channels), kernel[frame_lag], preferred_element_type=jnp.float32
        ).reshape(frames + 2, frame_rows * columns, -1)
        for frame_lag in range(3)
    ]
    conv = conv_bias + sum(
        spread_out[frame_lag][frame_lag : frame_lag + frames] for frame_lag in range(3)
    )
    conv = conv.reshape(frames, frame_rows, columns, -1)
    block_out = conv.astype(jnp.bfloat16)
    per_group = channels // GROUPS
    grouped = block_out.astype(jnp.float32).reshape(frames, frame_rows * columns, GROUPS, per_group)
    live_mask = live_frames[:, None, None, None]
    members = jnp.sum(live_frames) * (frame_rows * columns * per_group)
    first_sum = jnp.sum(grouped * live_mask, axis=(0, 1, 3))
    second_sum = jnp.sum(grouped * grouped * live_mask, axis=(0, 1, 3))
    clip_mean = first_sum / members
    clip_spread = second_sum / members - clip_mean * clip_mean
    clip_inverse = lax.rsqrt(clip_spread + eps)

    tiles = block_out.reshape(frames, NRB, tile_rows, columns, channels)
    tiles = jnp.pad(tiles, ((0, per_dest * classes - frames), (0, 0), (0, 0), (0, 0), (0, 0)))
    tiles = tiles.reshape(per_dest, classes, NRB, tile_rows, columns, channels)
    lag_of = (jnp.arange(classes, dtype=jnp.int32)[:, None] - (starts // NRB)[None, :] % classes) % classes
    pick = jnp.sum(jnp.where(clip_order[None, :] == device, lag_of, 0), axis=1)
    chosen = jnp.broadcast_to(tiles[:, 0:1], tiles.shape)
    for lag in range(1, classes):
        chosen = jnp.where(
            (pick == lag)[None, :, None, None, None, None], tiles[:, lag : lag + 1], chosen
        )
    tiles = chosen
    tiles = jnp.transpose(tiles, (1, 2, 3, 0, 4, 5)).reshape(
        devices, tile_rows * per_dest * columns, channels
    )
    stats = jnp.stack([clip_mean, clip_inverse], 0)
    stats = jnp.repeat(stats, per_group, axis=1)
    high = lax.reduce_precision(stats, exponent_bits=8, mantissa_bits=7)
    low = stats - high
    stat_rows = jnp.concatenate([high, low, jnp.zeros((4, channels), jnp.float32)], 0)
    stat_rows = jnp.broadcast_to(stat_rows.astype(jnp.bfloat16)[None], (devices, 8, channels))
    outgoing = jnp.concatenate([tiles, stat_rows], 1)
    received = lax.all_to_all(outgoing, "tile", split_axis=0, concat_axis=0, tiled=True)
    block_part = received[:, : per_dest * tile_rows * columns].reshape(
        devices, tile_rows, per_dest, columns, channels
    )
    stat_part = received[:, per_dest * tile_rows * columns :].astype(jnp.float32)
    src_mean = stat_part[:, 0] + stat_part[:, 2]
    src_inverse = stat_part[:, 1] + stat_part[:, 3]
    local_slot = jnp.arange(worker_tiles, dtype=jnp.int32)
    tile_id = local_slot * devices + device
    placed = jnp.sum((starts[None, :] <= tile_id[:, None]).astype(jnp.int32), axis=1) - 1
    at_place = placed[:, None] == positions[None, :]
    clip_id = jnp.sum(jnp.where(at_place, clip_order[None, :], 0), axis=1)
    within = tile_id - jnp.sum(jnp.where(at_place, starts[None, :], 0), axis=1)
    row_of = jnp.arange(tile_rows, dtype=jnp.int32)[:, None]
    take_from = (clip_id[None, :] * tile_rows + row_of) * per_dest + (within // NRB // classes)[None, :]
    rows_all = devices * tile_rows * per_dest
    block_mine = jnp.take(block_part.reshape(rows_all, columns, channels), take_from, axis=0, mode="clip")
    tile_mean = jnp.broadcast_to(src_mean[0], (worker_tiles, channels))
    tile_inverse = jnp.broadcast_to(src_inverse[0], (worker_tiles, channels))
    for source in range(1, devices):
        hit = (clip_id == source)[:, None]
        tile_mean = jnp.where(hit, src_mean[source], tile_mean)
        tile_inverse = jnp.where(hit, src_inverse[source], tile_inverse)
    normed_mine = (block_mine.astype(jnp.float32) - tile_mean[None, :, None, :]) * tile_inverse[
        None, :, None, :
    ] * out_scale + out_offset
    normed_mine = jax.nn.silu(normed_mine).astype(jnp.bfloat16)
    return (block_mine, normed_mine)


def solution(mesh):
    in_specs = (
        P(("grp", "tile"), None, None, None),
        P("grp"),
        P("grp"),
        P(),
        P(),
        P(),
        P(),
        P(),
        P(),
    )
    out_specs = (P(None, ("grp", "tile"), None, None), P(None, ("grp", "tile"), None, None))
    return jax.shard_map(local, mesh=mesh, in_specs=in_specs, out_specs=out_specs, check_vma=False)
```

```python
import jax
import jax.numpy as jnp
from jax import lax
from jax.sharding import PartitionSpec as P

GROUPS = 32
MEANF = 4
NRB = 8


eps = 1e-06


def normalize(values, live_frames, scaling, offsets):
    frames = values.shape[0]
    channels = values.shape[-1]
    flat = values.reshape(frames, -1, channels)
    live_mask = live_frames[:, None]
    members = jnp.sum(live_frames) * flat.shape[1] * (channels // GROUPS)
    first = jnp.sum(jnp.sum(flat, axis=1) * live_mask, axis=0)
    second = jnp.sum(jnp.sum(flat * flat, axis=1) * live_mask, axis=0)
    group_mean = jnp.sum(first.reshape(GROUPS, -1), axis=1) / members
    spread = jnp.sum(second.reshape(GROUPS, -1), axis=1) / members - group_mean * group_mean
    inverse = lax.rsqrt(spread + eps)
    grouped = values.reshape(frames, -1, GROUPS, channels // GROUPS)
    normed = (grouped - group_mean[:, None]) * inverse[:, None] * scaling.reshape(
        GROUPS, -1
    ) + offsets.reshape(GROUPS, -1)
    return jax.nn.silu(normed).reshape(values.shape)


def local(
    latents,
    frame_counts,
    clip_order,
    norm_scale,
    norm_offset,
    conv_weight,
    conv_bias,
    out_scale,
    out_offset,
):
    devices = lax.axis_size("tile")
    device = lax.axis_index("tile")
    frames, frame_rows, columns, channels = latents.shape
    tile_rows = frame_rows // NRB
    classes = devices // NRB
    per_dest = (frames + classes - 1) // classes
    worker_tiles = MEANF * NRB
    meta = lax.optimization_barrier(jnp.stack([frame_counts, clip_order], 0))
    frame_counts, clip_order = meta[0], meta[1]
    positions = jnp.arange(frame_counts.shape[0], dtype=jnp.int32)
    chosen = clip_order[:, None] == positions[None, :]
    ordered = jnp.sum(jnp.where(chosen, frame_counts[None, :], 0), axis=1)
    starts = (jnp.cumsum(ordered) - ordered) * NRB
    live_frames = jnp.sum(
        jnp.where(
            (positions[None, :] == device)
            & (jnp.arange(latents.shape[0], dtype=jnp.int32)[:, None] < frame_counts[None, :]),
            1.0,
            0.0,
        ),
        axis=1,
    )

    active = normalize(latents.astype(jnp.float32), live_frames, norm_scale, norm_offset).astype(
        jnp.bfloat16
    )
    padded = jnp.pad(active, ((0, 0), (1, 1), (1, 1), (0, 0)))
    unfolded = jnp.concatenate(
        [
            padded[:, row_tap : row_tap + frame_rows, col_tap : col_tap + columns]
            for row_tap in range(3)
            for col_tap in range(3)
        ],
        axis=-1,
    ).reshape(frames * frame_rows * columns, 9 * channels)
    kernel = conv_weight.reshape(3, 9 * channels, -1)
    spread_out = [
        jnp.pad(
            jnp.dot(unfolded, kernel[frame_lag], preferred_element_type=jnp.float32).reshape(
                frames, frame_rows * columns, -1
            ),
            ((2 - frame_lag, 0), (0, 0), (0, 0)),
        )[:frames]
        for frame_lag in range(3)
    ]
    conv = conv_bias + sum(spread_out)
    conv = conv.reshape(frames, frame_rows, columns, -1)
    block_out = conv.astype(jnp.bfloat16)
    per_group = channels // GROUPS
    grouped = block_out.astype(jnp.float32).reshape(frames, frame_rows * columns, GROUPS, per_group)
    live_mask = live_frames[:, None, None, None]
    members = jnp.sum(live_frames) * (frame_rows * columns * per_group)
    first_sum = jnp.sum(grouped * live_mask, axis=(0, 1, 3))
    second_sum = jnp.sum(grouped * grouped * live_mask, axis=(0, 1, 3))
    clip_mean = first_sum / members
    clip_spread = second_sum / members - clip_mean * clip_mean
    clip_inverse = lax.rsqrt(clip_spread + eps)

    tiles = block_out.reshape(frames, NRB, tile_rows, columns, channels)
    tiles = jnp.pad(tiles, ((0, per_dest * classes - frames), (0, 0), (0, 0), (0, 0), (0, 0)))
    tiles = tiles.reshape(per_dest, classes, NRB, tile_rows, columns, channels)
    lag_of = (jnp.arange(classes, dtype=jnp.int32)[:, None] - (starts // NRB)[None, :] % classes) % classes
    pick = jnp.sum(jnp.where(clip_order[None, :] == device, lag_of, 0), axis=1)
    chosen = jnp.broadcast_to(tiles[:, 0:1], tiles.shape)
    for lag in range(1, classes):
        chosen = jnp.where(
            (pick == lag)[None, :, None, None, None, None], tiles[:, lag : lag + 1], chosen
        )
    tiles = chosen
    tiles = jnp.transpose(tiles, (1, 2, 3, 0, 4, 5)).reshape(
        devices, tile_rows * per_dest * columns, channels
    )
    stats = jnp.stack([clip_mean, clip_inverse], 0)
    stats = jnp.repeat(stats, per_group, axis=1)
    high = lax.reduce_precision(stats, exponent_bits=8, mantissa_bits=7)
    low = stats - high
    stat_rows = jnp.concatenate([high, low, jnp.zeros((4, channels), jnp.float32)], 0)
    stat_rows = jnp.broadcast_to(stat_rows.astype(jnp.bfloat16)[None], (devices, 8, channels))
    outgoing = jnp.concatenate([tiles, stat_rows], 1)
    received = lax.all_to_all(outgoing, "tile", split_axis=0, concat_axis=0, tiled=True)
    block_part = received[:, : per_dest * tile_rows * columns].reshape(
        devices, tile_rows, per_dest, columns, channels
    )
    stat_part = received[:, per_dest * tile_rows * columns :].astype(jnp.float32)
    src_mean = stat_part[:, 0] + stat_part[:, 2]
    src_inverse = stat_part[:, 1] + stat_part[:, 3]
    local_slot = jnp.arange(worker_tiles, dtype=jnp.int32)
    tile_id = local_slot * devices + device
    placed = jnp.sum((starts[None, :] <= tile_id[:, None]).astype(jnp.int32), axis=1) - 1
    at_place = placed[:, None] == positions[None, :]
    clip_id = jnp.sum(jnp.where(at_place, clip_order[None, :], 0), axis=1)
    within = tile_id - jnp.sum(jnp.where(at_place, starts[None, :], 0), axis=1)
    row_of = jnp.arange(tile_rows, dtype=jnp.int32)[:, None]
    take_from = (clip_id[None, :] * tile_rows + row_of) * per_dest + (within // NRB // classes)[None, :]
    rows_all = devices * tile_rows * per_dest
    block_mine = jnp.take(block_part.reshape(rows_all, columns, channels), take_from, axis=0, mode="clip")
    tile_mean = jnp.broadcast_to(src_mean[0], (worker_tiles, channels))
    tile_inverse = jnp.broadcast_to(src_inverse[0], (worker_tiles, channels))
    for source in range(1, devices):
        hit = (clip_id == source)[:, None]
        tile_mean = jnp.where(hit, src_mean[source], tile_mean)
        tile_inverse = jnp.where(hit, src_inverse[source], tile_inverse)
    normed_mine = (block_mine.astype(jnp.float32) - tile_mean[None, :, None, :]) * tile_inverse[
        None, :, None, :
    ] * out_scale + out_offset
    normed_mine = jax.nn.silu(normed_mine).astype(jnp.bfloat16)
    return (block_mine, normed_mine)


def solution(mesh):
    in_specs = (
        P(("grp", "tile"), None, None, None),
        P("grp"),
        P("grp"),
        P(),
        P(),
        P(),
        P(),
        P(),
        P(),
    )
    out_specs = (P(None, ("grp", "tile"), None, None), P(None, ("grp", "tile"), None, None))
    return jax.shard_map(local, mesh=mesh, in_specs=in_specs, out_specs=out_specs, check_vma=False)
```

```python
import jax
import jax.numpy as jnp
from jax import lax
from jax.sharding import PartitionSpec as P

GROUPS = 32
MEANF = 4
NRB = 8


eps = 1e-06


def normalize(values, live_frames, scaling, offsets):
    frames = values.shape[0]
    channels = values.shape[-1]
    flat = values.reshape(frames, -1, channels)
    live_mask = live_frames[:, None]
    members = jnp.sum(live_frames) * flat.shape[1] * (channels // GROUPS)
    first = jnp.sum(jnp.sum(flat, axis=1) * live_mask, axis=0)
    second = jnp.sum(jnp.sum(flat * flat, axis=1) * live_mask, axis=0)
    group_mean = jnp.sum(first.reshape(GROUPS, -1), axis=1) / members
    spread = jnp.sum(second.reshape(GROUPS, -1), axis=1) / members - group_mean * group_mean
    inverse = lax.rsqrt(spread + eps)
    grouped = values.reshape(frames, -1, GROUPS, channels // GROUPS)
    normed = (grouped - group_mean[:, None]) * inverse[:, None] * scaling.reshape(
        GROUPS, -1
    ) + offsets.reshape(GROUPS, -1)
    return jax.nn.silu(normed).reshape(values.shape)


def local(
    latents,
    frame_counts,
    clip_order,
    norm_scale,
    norm_offset,
    conv_weight,
    conv_bias,
    out_scale,
    out_offset,
):
    devices = lax.axis_size("tile")
    device = lax.axis_index("tile")
    frames, frame_rows, columns, channels = latents.shape
    tile_rows = frame_rows // NRB
    classes = devices // NRB
    per_dest = (frames + classes - 1) // classes
    worker_tiles = MEANF * NRB
    meta = lax.optimization_barrier(jnp.stack([frame_counts, clip_order], 0))
    frame_counts, clip_order = meta[0], meta[1]
    positions = jnp.arange(frame_counts.shape[0], dtype=jnp.int32)
    chosen = clip_order[:, None] == positions[None, :]
    ordered = jnp.sum(jnp.where(chosen, frame_counts[None, :], 0), axis=1)
    starts = (jnp.cumsum(ordered) - ordered) * NRB
    live_frames = jnp.sum(
        jnp.where(
            (positions[None, :] == device)
            & (jnp.arange(latents.shape[0], dtype=jnp.int32)[:, None] < frame_counts[None, :]),
            1.0,
            0.0,
        ),
        axis=1,
    )

    active = normalize(latents.astype(jnp.float32), live_frames, norm_scale, norm_offset).astype(
        jnp.bfloat16
    )
    padded = jnp.pad(active, ((0, 0), (1, 1), (1, 1), (0, 0)))
    unfolded = jnp.concatenate(
        [
            padded[:, row_tap : row_tap + frame_rows, col_tap : col_tap + columns]
            for row_tap in range(3)
            for col_tap in range(3)
        ],
        axis=-1,
    ).reshape(frames * frame_rows * columns, 9 * channels)
    kernel = conv_weight.reshape(3, 9 * channels, -1)
    spread_out = [
        jnp.pad(
            jnp.dot(unfolded, kernel[frame_lag], preferred_element_type=jnp.float32).reshape(
                frames, frame_rows * columns, -1
            ),
            ((2 - frame_lag, 0), (0, 0), (0, 0)),
        )[:frames]
        for frame_lag in range(3)
    ]
    conv = conv_bias + sum(spread_out)
    conv = conv.reshape(frames, frame_rows, columns, -1)
    block_out = conv.astype(jnp.bfloat16)
    per_group = channels // GROUPS
    grouped = block_out.astype(jnp.float32).reshape(frames, frame_rows * columns, GROUPS, per_group)
    live_mask = live_frames[:, None, None, None]
    members = jnp.sum(live_frames) * (frame_rows * columns * per_group)
    first_sum = jnp.sum(grouped * live_mask, axis=(0, 1, 3))
    second_sum = jnp.sum(grouped * grouped * live_mask, axis=(0, 1, 3))
    clip_mean = first_sum / members
    clip_spread = second_sum / members - clip_mean * clip_mean
    clip_inverse = lax.rsqrt(clip_spread + eps)

    tiles = block_out.reshape(frames, NRB, tile_rows, columns, channels)
    tiles = jnp.pad(tiles, ((0, per_dest * classes - frames), (0, 0), (0, 0), (0, 0), (0, 0)))
    tiles = tiles.reshape(per_dest, classes, NRB, tile_rows, columns, channels)
    lag_of = (jnp.arange(classes, dtype=jnp.int32)[:, None] - (starts // NRB)[None, :] % classes) % classes
    pick = jnp.sum(jnp.where(clip_order[None, :] == device, lag_of, 0), axis=1)
    chosen = jnp.broadcast_to(tiles[:, 0:1], tiles.shape)
    for lag in range(1, classes):
        chosen = jnp.where(
            (pick == lag)[None, :, None, None, None, None], tiles[:, lag : lag + 1], chosen
        )
    tiles = chosen
    tiles = jnp.transpose(tiles, (1, 2, 3, 0, 4, 5)).reshape(
        devices, tile_rows * per_dest * columns, channels
    )
    stats = jnp.stack([clip_mean, clip_inverse], 0)
    stats = jnp.repeat(stats, per_group, axis=1)
    high = lax.reduce_precision(stats, exponent_bits=8, mantissa_bits=7)
    low = stats - high
    stat_rows = jnp.concatenate([high, low, jnp.zeros((4, channels), jnp.float32)], 0)
    stat_rows = jnp.broadcast_to(stat_rows.astype(jnp.bfloat16)[None], (devices, 8, channels))
    outgoing = jnp.concatenate([tiles, stat_rows], 1)
    received = lax.all_to_all(outgoing, "tile", split_axis=0, concat_axis=0, tiled=True)
    block_part = received[:, : per_dest * tile_rows * columns].reshape(
        devices, tile_rows, per_dest, columns, channels
    )
    stat_part = received[:, per_dest * tile_rows * columns :].astype(jnp.float32)
    src_mean = stat_part[:, 0] + stat_part[:, 2]
    src_inverse = stat_part[:, 1] + stat_part[:, 3]
    local_slot = jnp.arange(worker_tiles, dtype=jnp.int32)
    tile_id = local_slot * devices + device
    placed = jnp.sum((starts[None, :] <= tile_id[:, None]).astype(jnp.int32), axis=1) - 1
    at_place = placed[:, None] == positions[None, :]
    clip_id = jnp.sum(jnp.where(at_place, clip_order[None, :], 0), axis=1)
    within = tile_id - jnp.sum(jnp.where(at_place, starts[None, :], 0), axis=1)
    row_of = jnp.arange(tile_rows, dtype=jnp.int32)[:, None]
    take_from = (clip_id[None, :] * tile_rows + row_of) * per_dest + (within // NRB // classes)[None, :]
    rows_all = devices * tile_rows * per_dest
    block_mine = jnp.take(block_part.reshape(rows_all, columns, channels), take_from, axis=0, mode="clip")
    src_stats = jnp.stack([src_mean, src_inverse], 1)
    tile_stats = jnp.broadcast_to(src_stats[0], (worker_tiles, 2, channels))
    for source in range(1, devices):
        tile_stats = jnp.where((clip_id == source)[:, None, None], src_stats[source], tile_stats)
    tile_mean, tile_inverse = tile_stats[:, 0], tile_stats[:, 1]
    normed_mine = (block_mine.astype(jnp.float32) - tile_mean[None, :, None, :]) * tile_inverse[
        None, :, None, :
    ] * out_scale + out_offset
    normed_mine = jax.nn.silu(normed_mine).astype(jnp.bfloat16)
    return (block_mine, normed_mine)


def solution(mesh):
    in_specs = (
        P(("grp", "tile"), None, None, None),
        P("grp"),
        P("grp"),
        P(),
        P(),
        P(),
        P(),
        P(),
        P(),
    )
    out_specs = (P(None, ("grp", "tile"), None, None), P(None, ("grp", "tile"), None, None))
    return jax.shard_map(local, mesh=mesh, in_specs=in_specs, out_specs=out_specs, check_vma=False)
```
